32 devices in a mesh: pipe: 4 (over z), et: 8 (over y, x, core).
Axes of the slice: x: 2, y: 2, z: 4, core: 2. Of those that a mesh axis runs over, the one named last changes fastest.
Arguments:
- tokens: bfloat16 [4, 1024, 4096], P('pipe', 'et'), may hold values from -6 to 6
- gate_vals: bfloat16 [4, 1024, 2], P('pipe', 'et'), may hold values from 0.099609375 to 1
- expert_ids: int32 [4, 1024, 2], P('pipe', 'et'), may hold values from 0 to 7, as said below
- grad_out: bfloat16 [4, 1024, 4096], P('pipe', 'et'), may hold values from -6 to 6
- w_gate: bfloat16 [4, 2, 4096, 7168], P('pipe', None, None, 'et'), may hold values from -0.09375 to 0.09375
- w_up: bfloat16 [4, 2, 4096, 7168], P('pipe', None, None, 'et'), may hold values from -0.09375 to 0.09375
- w_down: bfloat16 [4, 2, 7168, 4096], P('pipe', None, 'et'), may hold values from -0.0625 to 0.0625
Outputs:
- moe_out: bfloat16 [4, 1024, 4096], P('pipe', 'et')
- prior_grads: bfloat16 [4, 1024, 4096], P('pipe', 'et')
The draws below stay inside these ranges and needn't reach their ends.
Inputs may be any that keep to these rules, and one draw needn't show every extreme that they name: `expert_ids`: each row names 2 different experts. The rows of one device of one section name each of experts 0 to 1 at most 16 times, and for each of these experts there is a section in which every device's rows name it exactly 16 times.
All inputs are finite; a program needn't handle non-finite values.
Results may differ from the reference program's by a relative error of at most 0.012.
Values may be sent and summed in bfloat16 or wider, within the bound.
No kernel may reach another device: no remote copies, remote signals or barrier semaphores. Data moves between devices by JAX's collectives and lax.ppermute only.
A program may use at most 192 MiB of HBM per device.

```python
import jax
import jax.numpy as jnp
from jax import lax

D = 4096
FF = 7168
EXPERTS = 8
TOP = 2
E_WIN = 2
TOK_DEV = 128
MOST = 16
PIPE = 4
TOKENS = 1024
CAP = 128
N_ET = 8


def draw_expert_ids(key, part):
    keys = jax.random.split(key, 7)
    blocks = TOKENS // TOK_DEV
    shape_three = (PIPE, blocks, TOK_DEV)
    counts = jax.random.randint(keys[0], (PIPE, blocks, 2), (MOST + 2) // 3, MOST + 1)
    full_section = jax.random.randint(keys[1], (2,), 0, PIPE)
    section_pos = jnp.arange(PIPE, dtype=jnp.int32)[:, None, None]
    counts = jnp.where(section_pos == full_section[None, None, :], MOST, counts)
    scores = jax.random.randint(keys[2], shape_three, 0, 1 << 20) * TOK_DEV + jnp.arange(TOK_DEV, dtype=jnp.int32)
    ranks = jnp.argsort(jnp.argsort(scores, axis=2), axis=2).astype(jnp.int32)
    offsets = jax.random.randint(keys[3], (PIPE, blocks, 1), 0, TOK_DEV)
    first_on = ranks < counts[..., 0:1]
    second_on = (ranks + offsets) % TOK_DEV < counts[..., 1:2]
    other_one = jax.random.randint(keys[4], shape_three, 2, EXPERTS)
    other_two = 2 + (other_one - 2 + jax.random.randint(keys[5], shape_three, 1, EXPERTS - 2)) % (EXPERTS - 2)
    slot_one = jnp.where(first_on, 0, other_one)
    slot_two = jnp.where(second_on, 1, other_two)
    flipped = jax.random.randint(keys[6], shape_three, 0, 2) == 1
    leading = jnp.where(flipped, slot_two, slot_one)
    trailing = jnp.where(flipped, slot_one, slot_two)
    return jnp.stack([leading, trailing], axis=-1).reshape(PIPE, TOKENS, 2).astype(jnp.int32)


def block_scale(rng, dims, cuts, low, top_value):
    factor_of = 1.0
    for dim, parts in cuts:
        heights = jax.random.uniform(jax.random.fold_in(jax.random.fold_in(rng, 6), dim), (parts,), jnp.float32, low / len(cuts), top_value / len(cuts))
        factor_of = factor_of * jnp.repeat(jnp.exp(heights), dims[dim] // parts).reshape((-1,) + (1,) * (len(dims) - 1 - dim))
    return factor_of


def centred(stream_key, extent, width, reach, pieces=(), kind=jnp.bfloat16):
    loudness = block_scale(stream_key, extent, pieces, -0.22, 0.18) if pieces else 1.0
    array = jax.random.normal(stream_key, extent, jnp.float32) * width * loudness
    return jnp.minimum(jnp.maximum(array, -reach), reach).astype(kind)


def setup_inputs(seed: int = 0) -> dict:
    arg_keys = jax.random.split(jax.random.key(seed), 8)
    return {
        "tokens": centred(arg_keys[0], (PIPE, TOKENS, D), 1.0, 6.0, ((0, 4), (1, 8))),
        "gate_vals": jnp.clip(0.099609375 + 0.9003906 * jax.random.uniform(arg_keys[1], (PIPE, TOKENS, TOP), jnp.float32) ** block_scale(arg_keys[1], (PIPE, TOKENS, TOP), ((0, 4), (1, 8)), -0.2, 0.2), 0.099609375, 1.0).astype(jnp.bfloat16),
        "expert_ids": draw_expert_ids(jax.random.fold_in(arg_keys[7], 71), 0),
        "grad_out": centred(arg_keys[3], (PIPE, TOKENS, D), 1.0, 6.0, ((0, 4), (1, 8))),
        "w_gate": centred(arg_keys[4], (PIPE, E_WIN, D, FF), D ** -0.5, 0.09375, ((0, 4), (3, 8))),
        "w_up": centred(arg_keys[5], (PIPE, E_WIN, D, FF), D ** -0.5, 0.09375, ((0, 4), (3, 8))),
        "w_down": centred(arg_keys[6], (PIPE, E_WIN, FF, D), FF ** -0.5, 0.0625, ((0, 4), (2, 8))),
    }


def silu_parts(pre_gate):
    sigma = jax.nn.sigmoid(pre_gate)
    return pre_gate * sigma, sigma * (1.0 + pre_gate * (1.0 - sigma))


def slot_layout(routed, groups, slot_width):
    length = routed.shape[0] // groups
    flags = routed.reshape(groups, length)
    positions = jnp.cumsum(flags.astype(jnp.int32), axis=1, dtype=jnp.int32) - 1
    positions = positions + (jnp.arange(groups, dtype=jnp.int32) * slot_width)[:, None]
    targets = jnp.where(flags, positions, groups * slot_width).reshape(-1).astype(jnp.int32)
    sources = jnp.zeros((groups * slot_width,), jnp.int32).at[targets].set(
        jnp.arange(groups * length, dtype=jnp.int32), mode="drop")
    return targets, sources


def expert_slots(route_rows, gate_rows, expert, capacity):
    matches = route_rows == expert
    routed = jnp.any(matches, axis=1)
    gate_val = jnp.sum(jnp.where(matches, gate_rows.astype(jnp.float32), 0.0), axis=1)
    targets, sources = slot_layout(routed, 1, capacity)
    weights = jnp.zeros((capacity,), jnp.float32).at[targets].set(gate_val, mode="drop")
    return sources, weights


def one_section(tok_rows, gate_rows, route_rows, grad_rows, gate_mats, up_mats, down_mats):
    slots = [expert_slots(route_rows, gate_rows, expert, CAP) for expert in range(E_WIN)]
    shard_cols = FF // N_ET

    def shard_step(shard_num, carry):
        out_tot, grad_tot = carry
        start = jnp.asarray(shard_num * shard_cols).astype(jnp.int32)
        out_acc = jnp.zeros((TOKENS, D), jnp.float32)
        grad_acc = jnp.zeros((TOKENS, D), jnp.float32)
        for expert in range(E_WIN):
            sources, weights = slots[expert]
            rows = tok_rows[sources]
            grads = grad_rows[sources]
            gate_cols = lax.dynamic_slice_in_dim(gate_mats[expert], start, shard_cols, 1)
            up_cols = lax.dynamic_slice_in_dim(up_mats[expert], start, shard_cols, 1)
            down_rows = lax.dynamic_slice_in_dim(down_mats[expert], start, shard_cols, 0)
            pre_gate = jnp.dot(rows, gate_cols, preferred_element_type=jnp.float32)
            pre_up = jnp.dot(rows, up_cols, preferred_element_type=jnp.float32)
            activated, slopes = silu_parts(pre_gate)
            hidden = (activated * pre_up).astype(jnp.bfloat16)
            out_acc = out_acc.at[sources].add(
                weights[:, None] * jnp.dot(hidden, down_rows, preferred_element_type=jnp.float32))
            d_hidden = weights[:, None] * jnp.dot(grads, down_rows.T, preferred_element_type=jnp.float32)
            d_gate = (d_hidden * pre_up * slopes).astype(jnp.bfloat16)
            d_up = (d_hidden * activated).astype(jnp.bfloat16)
            grad_acc = grad_acc.at[sources].add(
                jnp.dot(d_gate, gate_cols.T, preferred_element_type=jnp.float32)
                + jnp.dot(d_up, up_cols.T, preferred_element_type=jnp.float32))
        out_tot = out_tot + lax.optimization_barrier(out_acc.astype(jnp.bfloat16)).astype(jnp.float32)
        grad_tot = grad_tot + lax.optimization_barrier(grad_acc.astype(jnp.bfloat16)).astype(jnp.float32)
        return out_tot, grad_tot

    start_sums = (jnp.zeros((TOKENS, D), jnp.float32), jnp.zeros((TOKENS, D), jnp.float32))
    out_tot, grad_tot = lax.fori_loop(0, N_ET, shard_step, start_sums)
    return out_tot.astype(jnp.bfloat16), grad_tot.astype(jnp.bfloat16)


def reference(tokens, gate_vals, expert_ids, grad_out, w_gate, w_up, w_down):
    outputs = []
    gradients = []
    for section_num in range(PIPE):
        out_section, grad_section = one_section(tokens[section_num], gate_vals[section_num], expert_ids[section_num],
                                          grad_out[section_num], w_gate[section_num], w_up[section_num],
                                          w_down[section_num])
        outputs.append(out_section)
        gradients.append(grad_section)
    moe_out = jnp.stack(outputs)
    received = gradients[1:] + [jnp.zeros((TOKENS, D), jnp.bfloat16)]
    prior_grads = jnp.stack(received)
    return moe_out, prior_grads
```

```python
import jax
import jax.numpy as jnp
from jax import lax
from jax.sharding import PartitionSpec as P

E_WIN = 2
MOST = 16
TAIL = 128


def shifted(value, axis, steps):
    count = lax.axis_size(axis)
    first, last = (max(0, -steps), min(count, count - steps))
    return lax.ppermute(value, axis, [(source, source + steps) for source in range(first, last)])


def silu_parts(pre_gate):
    sigma = jax.nn.sigmoid(pre_gate)
    return (pre_gate * sigma, sigma * (1.0 + pre_gate * (1.0 - sigma)))


def local_slots(local_routes, local_gates):
    count = local_routes.shape[0]
    sources, weights, targets = [], [], []
    for expert in range(E_WIN):
        matches = local_routes == expert
        routed = jnp.any(matches, axis=1)
        gate_val = jnp.sum(jnp.where(matches, local_gates.astype(jnp.float32), 0.0), axis=1)
        positions = jnp.cumsum(routed.astype(jnp.int32), dtype=jnp.int32) - 1
        target = jnp.where(routed, positions, MOST)
        sources.append(
            jnp.zeros((MOST,), jnp.int32).at[target].set(jnp.arange(count, dtype=jnp.int32), mode="drop")
        )
        weights.append(jnp.zeros((MOST,), jnp.float32).at[target].set(gate_val, mode="drop"))
        targets.append(jnp.where(routed, positions + expert * MOST, E_WIN * MOST))
    return jnp.concatenate(sources), jnp.concatenate(weights), targets


def reduce_to_owner(parts, axis):
    n = lax.axis_size(axis)
    me = lax.axis_index(axis)
    total = jnp.take(parts, me, axis=0).astype(jnp.float32)
    for step in range(1, n):
        chunk = jnp.take(parts, (me + step) % n, axis=0)
        total = total + lax.ppermute(chunk, axis, [(s, (s + step) % n) for s in range(n)]).astype(jnp.float32)
    return total


def unpack(slot_sums, targets):
    padded = jnp.concatenate([slot_sums, jnp.zeros((1, slot_sums.shape[1]), jnp.float32)], axis=0)
    total = padded[targets[0]]
    for target in targets[1:]:
        total = total + padded[target]
    return total.astype(jnp.bfloat16)


def per_device(tokens, gate_vals, expert_ids, grad_out, w_gate, w_up, w_down):
    local_rows = tokens[0]
    local_grads = grad_out[0]
    gate_mats = w_gate[0]
    up_mats = w_up[0]
    down_mats = w_down[0]
    n = lax.axis_size("et")
    width = local_rows.shape[1]
    sources, weights, targets = local_slots(expert_ids[0], gate_vals[0])
    weight_cols = jnp.broadcast_to(weights.astype(jnp.bfloat16)[:, None], (E_WIN * MOST, TAIL))
    packed = jnp.concatenate([local_rows[sources], weight_cols], axis=1)
    all_rows = lax.all_gather(packed, "et", axis=0, tiled=True).reshape(n, E_WIN, MOST, width + TAIL)
    grads = lax.all_gather(local_grads[sources], "et", axis=0, tiled=True).reshape(n, E_WIN, MOST, width)
    outs = []
    stored = []
    for expert in range(E_WIN):
        rows = all_rows[:, expert, :, :width].reshape(n * MOST, width)
        gate_w = all_rows[:, expert, :, width].reshape(n * MOST, 1).astype(jnp.float32)
        pre_gate = jnp.dot(rows, gate_mats[expert], preferred_element_type=jnp.float32)
        pre_up = jnp.dot(rows, up_mats[expert], preferred_element_type=jnp.float32)
        activated, slopes = silu_parts(pre_gate)
        hidden = (activated * pre_up).astype(jnp.bfloat16)
        out_e = gate_w * jnp.dot(hidden, down_mats[expert], preferred_element_type=jnp.float32)
        outs.append(out_e.astype(jnp.bfloat16).reshape(n, MOST, width))
        stored.append((gate_w, pre_up, activated, slopes))
    out_parts = jnp.stack(outs, axis=1).reshape(n, E_WIN * MOST, width)
    out_share = unpack(reduce_to_owner(out_parts, "et"), targets)
    grad_outs = []
    for expert in range(E_WIN):
        gate_w, pre_up, activated, slopes = stored[expert]
        grad_rows = grads[:, expert].reshape(n * MOST, width)
        d_hidden = gate_w * lax.dot_general(
            grad_rows, down_mats[expert], (((1,), (1,)), ((), ())), preferred_element_type=jnp.float32
        )
        d_gate = (d_hidden * pre_up * slopes).astype(jnp.bfloat16)
        d_up = (d_hidden * activated).astype(jnp.bfloat16)
        grad_e = lax.dot_general(
            d_gate, gate_mats[expert], (((1,), (1,)), ((), ())), preferred_element_type=jnp.float32
        ) + lax.dot_general(d_up, up_mats[expert], (((1,), (1,)), ((), ())), preferred_element_type=jnp.float32)
        grad_outs.append(grad_e.astype(jnp.bfloat16).reshape(n, MOST, width))
    grad_parts = jnp.stack(grad_outs, axis=1).reshape(n, E_WIN * MOST, width)
    grad_share = unpack(reduce_to_owner(grad_parts, "et"), targets)
    received = shifted(grad_share, "pipe", -1)
    return (out_share[None], received[None])


def solution(mesh):
    placed = (
        P("pipe", "et", None),
        P("pipe", "et", None),
        P("pipe", "et", None),
        P("pipe", "et", None),
        P("pipe", None, None, "et"),
        P("pipe", None, None, "et"),
        P("pipe", None, "et", None),
    )
    return jax.shard_map(
        per_device,
        mesh=mesh,
        in_specs=placed,
        out_specs=(P("pipe", "et", None), P("pipe", "et", None)),
        check_vma=False,
    )
```

```python
import jax
import jax.numpy as jnp
from jax import lax
from jax.sharding import PartitionSpec as P

E_WIN = 2
MOST = 16
TAIL = 128


def shifted(value, axis, steps):
    count = lax.axis_size(axis)
    first, last = (max(0, -steps), min(count, count - steps))
    return lax.ppermute(value, axis, [(source, source + steps) for source in range(first, last)])


def silu_parts(pre_gate):
    sigma = jax.nn.sigmoid(pre_gate)
    return (pre_gate * sigma, sigma * (1.0 + pre_gate * (1.0 - sigma)))


def local_slots(local_routes, local_gates):
    count = local_routes.shape[0]
    sources, weights, targets = [], [], []
    for expert in range(E_WIN):
        matches = local_routes == expert
        routed = jnp.any(matches, axis=1)
        gate_val = jnp.sum(jnp.where(matches, local_gates.astype(jnp.float32), 0.0), axis=1)
        positions = jnp.minimum(jnp.cumsum(routed.astype(jnp.int32), dtype=jnp.int32) - 1, MOST)
        target = jnp.where(routed, positions, MOST)
        sources.append(
            jnp.zeros((MOST,), jnp.int32).at[target].set(jnp.arange(count, dtype=jnp.int32), mode="drop")
        )
        weights.append(jnp.zeros((MOST,), jnp.float32).at[target].set(gate_val, mode="drop"))
        targets.append(jnp.where(routed & (positions < MOST), positions + expert * MOST, E_WIN * MOST))
    return jnp.concatenate(sources), jnp.concatenate(weights), targets


def reduce_to_previous(parts):
    n = lax.axis_size("et")
    stages = lax.axis_size("pipe")
    me = lax.axis_index("et")
    total = None
    for step in range(n):
        chunk = jnp.take(parts, (me + step) % n, axis=0)
        pairs = [
            (stage * n + source, (stage - 1) * n + (source + step) % n)
            for stage in range(1, stages)
            for source in range(n)
        ]
        moved = lax.ppermute(chunk, ("pipe", "et"), pairs).astype(jnp.float32)
        total = moved if total is None else total + moved
    return total


def unpack(slot_sums, targets):
    padded = jnp.concatenate([slot_sums, jnp.zeros((1, slot_sums.shape[1]), jnp.float32)], axis=0)
    total = padded[targets[0]]
    for target in targets[1:]:
        total = total + padded[target]
    return total.astype(jnp.bfloat16)


def per_device(tokens, gate_vals, expert_ids, grad_out, w_gate, w_up, w_down):
    local_rows = tokens[0]
    local_grads = grad_out[0]
    gate_mats = w_gate[0]
    up_mats = w_up[0]
    down_mats = w_down[0]
    n = lax.axis_size("et")
    width = local_rows.shape[1]
    sources, weights, targets = local_slots(expert_ids[0], gate_vals[0])
    next_routes = shifted(expert_ids[0], "pipe", -1)
    next_targets = local_slots(next_routes, gate_vals[0])[2]
    weight_cols = jnp.broadcast_to(weights.astype(jnp.bfloat16)[:, None], (E_WIN * MOST, TAIL))
    packed = jnp.concatenate([local_rows[sources], weight_cols], axis=1)
    all_rows = lax.all_gather(packed, "et", axis=0, tiled=True).reshape(n, E_WIN, MOST, width + TAIL)
    first_gate = jnp.dot(all_rows[:, 0, :, :width].reshape(n * MOST, width), gate_mats[0], preferred_element_type=jnp.float32)
    grad_rows_local, first_gate = lax.optimization_barrier((local_grads[sources], first_gate))
    grads = lax.all_gather(grad_rows_local, "et", axis=0, tiled=True).reshape(n, E_WIN, MOST, width)
    outs = []
    stored = []
    for expert in range(E_WIN):
        rows = all_rows[:, expert, :, :width].reshape(n * MOST, width)
        gate_w = all_rows[:, expert, :, width].reshape(n * MOST, 1).astype(jnp.float32)
        pre_gate = first_gate if expert == 0 else jnp.dot(rows, gate_mats[expert], preferred_element_type=jnp.float32)
        pre_up = jnp.dot(rows, up_mats[expert], preferred_element_type=jnp.float32)
        activated, slopes = silu_parts(pre_gate)
        hidden = (activated * pre_up).astype(jnp.bfloat16)
        out_e = gate_w * jnp.dot(hidden, down_mats[expert], preferred_element_type=jnp.float32)
        outs.append(out_e.astype(jnp.bfloat16).reshape(n, MOST, width))
        stored.append((gate_w, pre_up, activated, slopes))
    out_parts = jnp.stack(outs, axis=1).reshape(n, E_WIN * MOST, width)
    out_sums = lax.psum_scatter(out_parts.reshape(n * E_WIN * MOST, width), "et", scatter_dimension=0, tiled=True)
    out_share = unpack(out_sums.astype(jnp.float32), targets)
    grad_outs = []
    for expert in range(E_WIN):
        gate_w, pre_up, activated, slopes = stored[expert]
        grad_rows = grads[:, expert].reshape(n * MOST, width)
        d_hidden = gate_w * lax.dot_general(
            grad_rows, down_mats[expert], (((1,), (1,)), ((), ())), preferred_element_type=jnp.float32
        )
        d_gate = (d_hidden * pre_up * slopes).astype(jnp.bfloat16)
        d_up = (d_hidden * activated).astype(jnp.bfloat16)
        grad_e = lax.dot_general(
            d_gate, gate_mats[expert], (((1,), (1,)), ((), ())), preferred_element_type=jnp.float32
        ) + lax.dot_general(d_up, up_mats[expert], (((1,), (1,)), ((), ())), preferred_element_type=jnp.float32)
        grad_outs.append(grad_e.astype(jnp.bfloat16).reshape(n, MOST, width))
    grad_parts = jnp.stack(grad_outs, axis=1).reshape(n, E_WIN * MOST, width)
    received = unpack(reduce_to_previous(grad_parts), next_targets)
    return (out_share[None], received[None])


def solution(mesh):
    placed = (
        P("pipe", "et", None),
        P("pipe", "et", None),
        P("pipe", "et", None),
        P("pipe", "et", None),
        P("pipe", None, None, "et"),
        P("pipe", None, None, "et"),
        P("pipe", None, "et", None),
    )
    return jax.shard_map(
        per_device,
        mesh=mesh,
        in_specs=placed,
        out_specs=(P("pipe", "et", None), P("pipe", "et", None)),
        check_vma=False,
    )
```

```python
import jax
import jax.numpy as jnp
from jax import lax
from jax.sharding import PartitionSpec as P

E_WIN = 2
MOST = 16
TAIL = 128


def shifted(value, axis, steps):
    count = lax.axis_size(axis)
    first, last = (max(0, -steps), min(count, count - steps))
    return lax.ppermute(value, axis, [(source, source + steps) for source in range(first, last)])


def silu_parts(pre_gate):
    sigma = jax.nn.sigmoid(pre_gate)
    return (pre_gate * sigma, sigma * (1.0 + pre_gate * (1.0 - sigma)))


def local_slots(local_routes, local_gates):
    slot_ids = jnp.arange(MOST, dtype=jnp.int32)[:, None]
    selects, weights = [], []
    for expert in range(E_WIN):
        matches = local_routes == expert
        routed = jnp.any(matches, axis=1)
        gate_val = jnp.sum(jnp.where(matches, local_gates.astype(jnp.float32), 0.0), axis=1)
        positions = jnp.cumsum(routed.astype(jnp.int32), dtype=jnp.int32) - 1
        select = routed[None, :] & (positions[None, :] == slot_ids)
        selects.append(select)
        weights.append(jnp.sum(jnp.where(select, gate_val[None, :], 0.0), axis=1))
    return jnp.concatenate(selects, axis=0), jnp.concatenate(weights)


def pick_rows(select, rows):
    return jnp.dot(select.astype(rows.dtype), rows, preferred_element_type=jnp.float32).astype(rows.dtype)


def reduce_to_previous(parts):
    n = lax.axis_size("et")
    stages = lax.axis_size("pipe")
    me = lax.axis_index("et")
    total = None
    for step in range(n):
        chunk = jnp.take(parts, (me + step) % n, axis=0)
        pairs = [
            (stage * n + source, (stage - 1) * n + (source + step) % n)
            for stage in range(1, stages)
            for source in range(n)
        ]
        moved = lax.ppermute(chunk, ("pipe", "et"), pairs).astype(jnp.float32)
        total = moved if total is None else total + moved
    return total


def unpack(slot_sums, select):
    return lax.dot_general(
        select.astype(jnp.float32),
        slot_sums,
        (((0,), (0,)), ((), ())),
        precision=lax.Precision.HIGHEST,
        preferred_element_type=jnp.float32,
    ).astype(jnp.bfloat16)


def per_device(tokens, gate_vals, expert_ids, grad_out, w_gate, w_up, w_down):
    local_rows = tokens[0]
    local_grads = grad_out[0]
    gate_mats = w_gate[0]
    up_mats = w_up[0]
    down_mats = w_down[0]
    n = lax.axis_size("et")
    width = local_rows.shape[1]
    select, weights = local_slots(expert_ids[0], gate_vals[0])
    next_routes = shifted(expert_ids[0], "pipe", -1)
    next_select = local_slots(next_routes, gate_vals[0])[0]
    weight_cols = jnp.broadcast_to(weights.astype(jnp.bfloat16)[:, None], (E_WIN * MOST, TAIL))
    packed = jnp.concatenate([pick_rows(select, local_rows), weight_cols], axis=1)
    all_rows = lax.all_gather(packed, "et", axis=0, tiled=True).reshape(n, E_WIN, MOST, width + TAIL)
    first_gate = jnp.dot(all_rows[:, 0, :, :width].reshape(n * MOST, width), gate_mats[0], preferred_element_type=jnp.float32)
    grad_rows_local, first_gate = lax.optimization_barrier((pick_rows(select, local_grads), first_gate))
    grads = lax.all_gather(grad_rows_local, "et", axis=0, tiled=True).reshape(n, E_WIN, MOST, width)
    outs = []
    stored = []
    for expert in range(E_WIN):
        rows = all_rows[:, expert, :, :width].reshape(n * MOST, width)
        gate_w = all_rows[:, expert, :, width].reshape(n * MOST, 1).astype(jnp.float32)
        pre_gate = first_gate if expert == 0 else jnp.dot(rows, gate_mats[expert], preferred_element_type=jnp.float32)
        pre_up = jnp.dot(rows, up_mats[expert], preferred_element_type=jnp.float32)
        activated, slopes = silu_parts(pre_gate)
        hidden = (activated * pre_up).astype(jnp.bfloat16)
        out_e = gate_w * jnp.dot(hidden, down_mats[expert], preferred_element_type=jnp.float32)
        outs.append(out_e.astype(jnp.bfloat16).reshape(n, MOST, width))
        stored.append((gate_w, pre_up, activated, slopes))
    out_parts = jnp.stack(outs, axis=1).reshape(n, E_WIN * MOST, width)
    out_sums = lax.psum_scatter(out_parts.reshape(n * E_WIN * MOST, width), "et", scatter_dimension=0, tiled=True)
    out_share = unpack(out_sums.astype(jnp.float32), select)
    grad_outs = []
    for expert in range(E_WIN):
        gate_w, pre_up, activated, slopes = stored[expert]
        grad_rows = grads[:, expert].reshape(n * MOST, width)
        d_hidden = gate_w * lax.dot_general(
            grad_rows, down_mats[expert], (((1,), (1,)), ((), ())), preferred_element_type=jnp.float32
        )
        d_gate = (d_hidden * pre_up * slopes).astype(jnp.bfloat16)
        d_up = (d_hidden * activated).astype(jnp.bfloat16)
        grad_e = lax.dot_general(
            d_gate, gate_mats[expert], (((1,), (1,)), ((), ())), preferred_element_type=jnp.float32
        ) + lax.dot_general(d_up, up_mats[expert], (((1,), (1,)), ((), ())), preferred_element_type=jnp.float32)
        grad_outs.append(grad_e.astype(jnp.bfloat16).reshape(n, MOST, width))
    grad_parts = jnp.stack(grad_outs, axis=1).reshape(n, E_WIN * MOST, width)
    received = unpack(reduce_to_previous(grad_parts), next_select)
    return (out_share[None], received[None])


def solution(mesh):
    placed = (
        P("pipe", "et", None),
        P("pipe", "et", None),
        P("pipe", "et", None),
        P("pipe", "et", None),
        P("pipe", None, None, "et"),
        P("pipe", None, None, "et"),
        P("pipe", None, "et", None),
    )
    return jax.shard_map(
        per_device,
        mesh=mesh,
        in_specs=placed,
        out_specs=(P("pipe", "et", None), P("pipe", "et", None)),
        check_vma=False,
    )
```

```python
import jax
import jax.numpy as jnp
from jax import lax
from jax.sharding import PartitionSpec as P

E_WIN = 2
MOST = 16
TAIL = 128


def shifted(value, axis, steps):
    count = lax.axis_size(axis)
    first, last = (max(0, -steps), min(count, count - steps))
    return lax.ppermute(value, axis, [(source, source + steps) for source in range(first, last)])


def silu_parts(pre_gate):
    sigma = jax.nn.sigmoid(pre_gate)
    return (pre_gate * sigma, sigma * (1.0 + pre_gate * (1.0 - sigma)))


def local_slots(local_routes, local_gates):
    slot_ids = jnp.arange(MOST, dtype=jnp.int32)[:, None]
    selects, weights = [], []
    for expert in range(E_WIN):
        matches = local_routes == expert
        routed = jnp.any(matches, axis=1)
        gate_val = jnp.sum(jnp.where(matches, local_gates.astype(jnp.float32), 0.0), axis=1)
        positions = jnp.cumsum(routed.astype(jnp.int32), dtype=jnp.int32) - 1
        select = routed[None, :] & (positions[None, :] == slot_ids)
        selects.append(select)
        weights.append(jnp.sum(jnp.where(select, gate_val[None, :], 0.0), axis=1))
    return jnp.concatenate(selects, axis=0), jnp.concatenate(weights)


def pick_rows(select, rows):
    return jnp.dot(select.astype(rows.dtype), rows, preferred_element_type=jnp.float32).astype(rows.dtype)


def reduce_to_previous(parts):
    n = lax.axis_size("et")
    stages = lax.axis_size("pipe")
    me = lax.axis_index("et")
    held = parts
    bit = 1
    while 2 * bit < n:
        halves = held.reshape((held.shape[0] // 2, 2) + held.shape[1:])
        side = (me // bit) % 2
        keep = jnp.take(halves, side, axis=1)
        give = jnp.take(halves, 1 - side, axis=1)
        got = lax.ppermute(give, "et", [(i, i ^ bit) for i in range(n)])
        held = (keep.astype(jnp.float32) + got.astype(jnp.float32)).astype(jnp.bfloat16)
        bit *= 2
    side = (me // bit) % 2
    keep = jnp.take(held, side, axis=0)
    give = jnp.take(held, 1 - side, axis=0)
    to_same = [(stage * n + i, (stage - 1) * n + i) for stage in range(1, stages) for i in range(n)]
    to_other = [(stage * n + i, (stage - 1) * n + (i ^ bit)) for stage in range(1, stages) for i in range(n)]
    first = lax.ppermute(keep, ("pipe", "et"), to_same)
    second = lax.ppermute(give, ("pipe", "et"), to_other)
    return first.astype(jnp.float32) + second.astype(jnp.float32)


def unpack(slot_sums, select):
    return lax.dot_general(
        select.astype(jnp.float32),
        slot_sums,
        (((0,), (0,)), ((), ())),
        precision=lax.Precision.HIGHEST,
        preferred_element_type=jnp.float32,
    ).astype(jnp.bfloat16)


def per_device(tokens, gate_vals, expert_ids, grad_out, w_gate, w_up, w_down):
    local_rows = tokens[0]
    local_grads = grad_out[0]
    gate_mats = w_gate[0]
    up_mats = w_up[0]
    down_mats = w_down[0]
    n = lax.axis_size("et")
    width = local_rows.shape[1]
    select, weights = local_slots(expert_ids[0], gate_vals[0])
    next_routes = shifted(expert_ids[0], "pipe", -1)
    next_select = local_slots(next_routes, gate_vals[0])[0]
    weight_cols = jnp.broadcast_to(weights.astype(jnp.bfloat16)[:, None], (E_WIN * MOST, TAIL))
    packed = jnp.concatenate([pick_rows(select, local_rows), weight_cols], axis=1)
    all_rows = lax.all_gather(packed, "et", axis=0, tiled=True).reshape(n, E_WIN, MOST, width + TAIL)
    first_gate = jnp.dot(all_rows[:, 0, :, :width].reshape(n * MOST, width), gate_mats[0], preferred_element_type=jnp.float32)
    grad_rows_local, first_gate = lax.optimization_barrier((pick_rows(select, local_grads), first_gate))
    grads = lax.all_gather(grad_rows_local, "et", axis=0, tiled=True).reshape(n, E_WIN, MOST, width)
    outs = []
    stored = []
    for expert in range(E_WIN):
        rows = all_rows[:, expert, :, :width].reshape(n * MOST, width)
        gate_w = all_rows[:, expert, :, width].reshape(n * MOST, 1).astype(jnp.float32)
        pre_gate = first_gate if expert == 0 else jnp.dot(rows, gate_mats[expert], preferred_element_type=jnp.float32)
        pre_up = jnp.dot(rows, up_mats[expert], preferred_element_type=jnp.float32)
        activated, slopes = silu_parts(pre_gate)
        hidden = (activated * pre_up).astype(jnp.bfloat16)
        out_e = gate_w * jnp.dot(hidden, down_mats[expert], preferred_element_type=jnp.float32)
        outs.append(out_e.astype(jnp.bfloat16).reshape(n, MOST, width))
        stored.append((gate_w, pre_up, activated, slopes))
    out_parts = jnp.stack(outs, axis=1).reshape(n, E_WIN * MOST, width)
    out_sums = lax.psum_scatter(out_parts.reshape(n * E_WIN * MOST, width), "et", scatter_dimension=0, tiled=True)
    out_share = unpack(out_sums.astype(jnp.float32), select)
    grad_outs = []
    for expert in range(E_WIN):
        gate_w, pre_up, activated, slopes = stored[expert]
        grad_rows = grads[:, expert].reshape(n * MOST, width)
        d_hidden = gate_w * lax.dot_general(
            grad_rows, down_mats[expert], (((1,), (1,)), ((), ())), preferred_element_type=jnp.float32
        )
        d_gate = (d_hidden * pre_up * slopes).astype(jnp.bfloat16)
        d_up = (d_hidden * activated).astype(jnp.bfloat16)
        grad_e = lax.dot_general(
            d_gate, gate_mats[expert], (((1,), (1,)), ((), ())), preferred_element_type=jnp.float32
        ) + lax.dot_general(d_up, up_mats[expert], (((1,), (1,)), ((), ())), preferred_element_type=jnp.float32)
        grad_outs.append(grad_e.astype(jnp.bfloat16).reshape(n, MOST, width))
    grad_parts = jnp.stack(grad_outs, axis=1).reshape(n, E_WIN * MOST, width)
    received = unpack(reduce_to_previous(grad_parts), next_select)
    return (out_share[None], received[None])


def solution(mesh):
    placed = (
        P("pipe", "et", None),
        P("pipe", "et", None),
        P("pipe", "et", None),
        P("pipe", "et", None),
        P("pipe", None, None, "et"),
        P("pipe", None, None, "et"),
        P("pipe", None, "et", None),
    )
    return jax.shard_map(
        per_device,
        mesh=mesh,
        in_specs=placed,
        out_specs=(P("pipe", "et", None), P("pipe", "et", None)),
        check_vma=False,
    )
```

```python
import jax
import jax.numpy as jnp
from jax import lax
from jax.sharding import PartitionSpec as P

E_WIN = 2
MOST = 16
TAIL = 128


def shifted(value, axis, steps):
    count = lax.axis_size(axis)
    first, last = (max(0, -steps), min(count, count - steps))
    return lax.ppermute(value, axis, [(source, source + steps) for source in range(first, last)])


def silu_parts(pre_gate):
    sigma = jax.nn.sigmoid(pre_gate)
    return (pre_gate * sigma, sigma * (1.0 + pre_gate * (1.0 - sigma)))


def local_slots(local_routes, local_gates):
    slot_ids = jnp.arange(MOST, dtype=jnp.int32)[:, None]
    selects, weights = [], []
    for expert in range(E_WIN):
        matches = local_routes == expert
        routed = jnp.any(matches, axis=1)
        gate_val = jnp.sum(jnp.where(matches, local_gates.astype(jnp.float32), 0.0), axis=1)
        positions = jnp.cumsum(routed.astype(jnp.int32), dtype=jnp.int32) - 1
        select = routed[None, :] & (positions[None, :] == slot_ids)
        selects.append(select)
        weights.append(jnp.sum(jnp.where(select, gate_val[None, :], 0.0), axis=1))
    return jnp.concatenate(selects, axis=0), jnp.concatenate(weights)


def pick_rows(select, rows):
    return jnp.dot(select.astype(rows.dtype), rows, preferred_element_type=jnp.float32).astype(rows.dtype)


def halve_over_et(parts):
    n = lax.axis_size("et")
    me = lax.axis_index("et")
    held = parts
    bit = 1
    while 2 * bit < n:
        halves = held.reshape((held.shape[0] // 2, 2) + held.shape[1:])
        side = (me // bit) % 2
        keep = jnp.take(halves, side, axis=1)
        give = jnp.take(halves, 1 - side, axis=1)
        got = lax.ppermute(give, "et", [(i, i ^ bit) for i in range(n)])
        held = (keep.astype(jnp.float32) + got.astype(jnp.float32)).astype(jnp.bfloat16)
        bit *= 2
    side = (me // bit) % 2
    return jnp.take(held, side, axis=0), jnp.take(held, 1 - side, axis=0), bit


def reduce_to_owner(parts):
    n = lax.axis_size("et")
    keep, give, bit = halve_over_et(parts)
    got = lax.ppermute(give, "et", [(i, i ^ bit) for i in range(n)])
    return keep.astype(jnp.float32) + got.astype(jnp.float32)


def reduce_to_previous(parts):
    n = lax.axis_size("et")
    stages = lax.axis_size("pipe")
    keep, give, bit = halve_over_et(parts)
    to_same = [(stage * n + i, (stage - 1) * n + i) for stage in range(1, stages) for i in range(n)]
    to_other = [(stage * n + i, (stage - 1) * n + (i ^ bit)) for stage in range(1, stages) for i in range(n)]
    first = lax.ppermute(keep, ("pipe", "et"), to_same)
    second = lax.ppermute(give, ("pipe", "et"), to_other)
    return first.astype(jnp.float32) + second.astype(jnp.float32)


def unpack(slot_sums, select):
    return lax.dot_general(
        select.astype(jnp.float32),
        slot_sums,
        (((0,), (0,)), ((), ())),
        precision=lax.Precision.HIGHEST,
        preferred_element_type=jnp.float32,
    ).astype(jnp.bfloat16)


def per_device(tokens, gate_vals, expert_ids, grad_out, w_gate, w_up, w_down):
    local_rows = tokens[0]
    local_grads = grad_out[0]
    gate_mats = w_gate[0]
    up_mats = w_up[0]
    down_mats = w_down[0]
    n = lax.axis_size("et")
    width = local_rows.shape[1]
    select, weights = local_slots(expert_ids[0], gate_vals[0])
    next_routes = shifted(expert_ids[0], "pipe", -1)
    next_select = local_slots(next_routes, gate_vals[0])[0]
    weight_cols = jnp.broadcast_to(weights.astype(jnp.bfloat16)[:, None], (E_WIN * MOST, TAIL))
    packed = jnp.concatenate([pick_rows(select, local_rows), weight_cols], axis=1)
    all_rows = lax.all_gather(packed, "et", axis=0, tiled=True).reshape(n, E_WIN, MOST, width + TAIL)
    first_gate = jnp.dot(all_rows[:, 0, :, :width].reshape(n * MOST, width), gate_mats[0], preferred_element_type=jnp.float32)
    grad_rows_local, first_gate = lax.optimization_barrier((pick_rows(select, local_grads), first_gate))
    grads = lax.all_gather(grad_rows_local, "et", axis=0, tiled=True).reshape(n, E_WIN, MOST, width)
    outs = []
    stored = []
    for expert in range(E_WIN):
        rows = all_rows[:, expert, :, :width].reshape(n * MOST, width)
        gate_w = all_rows[:, expert, :, width].reshape(n * MOST, 1).astype(jnp.float32)
        pre_gate = first_gate if expert == 0 else jnp.dot(rows, gate_mats[expert], preferred_element_type=jnp.float32)
        pre_up = jnp.dot(rows, up_mats[expert], preferred_element_type=jnp.float32)
        activated, slopes = silu_parts(pre_gate)
        hidden = (activated * pre_up).astype(jnp.bfloat16)
        out_e = gate_w * jnp.dot(hidden, down_mats[expert], preferred_element_type=jnp.float32)
        outs.append(out_e.astype(jnp.bfloat16).reshape(n, MOST, width))
        stored.append((gate_w, pre_up, activated, slopes))
    out_parts = jnp.stack(outs, axis=1).reshape(n, E_WIN * MOST, width)
    out_sums = reduce_to_owner(out_parts)
    grad_outs = []
    for expert in range(E_WIN):
        gate_w, pre_up, activated, slopes = stored[expert]
        grad_rows = grads[:, expert].reshape(n * MOST, width)
        if expert == E_WIN - 1:
            out_sums, grad_rows = lax.optimization_barrier((out_sums, grad_rows))
        d_hidden = gate_w * lax.dot_general(
            grad_rows, down_mats[expert], (((1,), (1,)), ((), ())), preferred_element_type=jnp.float32
        )
        d_gate = (d_hidden * pre_up * slopes).astype(jnp.bfloat16)
        d_up = (d_hidden * activated).astype(jnp.bfloat16)
        grad_e = lax.dot_general(
            d_gate, gate_mats[expert], (((1,), (1,)), ((), ())), preferred_element_type=jnp.float32
        ) + lax.dot_general(d_up, up_mats[expert], (((1,), (1,)), ((), ())), preferred_element_type=jnp.float32)
        grad_outs.append(grad_e.astype(jnp.bfloat16).reshape(n, MOST, width))
    grad_parts = jnp.stack(grad_outs, axis=1).reshape(n, E_WIN * MOST, width)
    received = unpack(reduce_to_previous(grad_parts), next_select)
    out_share = unpack(out_sums, select)
    return (out_share[None], received[None])


def solution(mesh):
    placed = (
        P("pipe", "et", None),
        P("pipe", "et", None),
        P("pipe", "et", None),
        P("pipe", "et", None),
        P("pipe", None, None, "et"),
        P("pipe", None, None, "et"),
        P("pipe", None, "et", None),
    )
    return jax.shard_map(
        per_device,
        mesh=mesh,
        in_specs=placed,
        out_specs=(P("pipe", "et", None), P("pipe", "et", None)),
        check_vma=False,
    )
```

```python
import jax
import jax.numpy as jnp
from jax import lax
from jax.sharding import PartitionSpec as P

E_WIN = 2
MOST = 16
TAIL = 128


def shifted(value, axis, steps):
    count = lax.axis_size(axis)
    first, last = (max(0, -steps), min(count, count - steps))
    return lax.ppermute(value, axis, [(source, source + steps) for source in range(first, last)])


def silu_parts(pre_gate):
    sigma = jax.nn.sigmoid(pre_gate)
    return (pre_gate * sigma, sigma * (1.0 + pre_gate * (1.0 - sigma)))


def local_slots(local_routes, local_gates):
    slot_ids = jnp.arange(MOST, dtype=jnp.int32)[:, None]
    selects, weights = [], []
    for expert in range(E_WIN):
        matches = local_routes == expert
        routed = jnp.any(matches, axis=1)
        gate_val = jnp.sum(jnp.where(matches, local_gates.astype(jnp.float32), 0.0), axis=1)
        positions = jnp.cumsum(routed.astype(jnp.int32), dtype=jnp.int32) - 1
        select = routed[None, :] & (positions[None, :] == slot_ids)
        selects.append(select)
        weights.append(jnp.sum(jnp.where(select, gate_val[None, :], 0.0), axis=1))
    return jnp.concatenate(selects, axis=0), jnp.concatenate(weights)


def pick_rows(select, rows):
    return jnp.dot(select.astype(rows.dtype), rows, preferred_element_type=jnp.float32).astype(rows.dtype)


def halve_over_et(parts):
    n = lax.axis_size("et")
    me = lax.axis_index("et")
    held = parts
    bit = 1
    while 2 * bit < n:
        halves = held.reshape((held.shape[0] // 2, 2) + held.shape[1:])
        side = (me // bit) % 2
        keep = jnp.take(halves, side, axis=1)
        give = jnp.take(halves, 1 - side, axis=1)
        got = lax.ppermute(give, "et", [(i, i ^ bit) for i in range(n)])
        held = (keep.astype(jnp.float32) + got.astype(jnp.float32)).astype(jnp.bfloat16)
        bit *= 2
    side = (me // bit) % 2
    return jnp.take(held, side, axis=0), jnp.take(held, 1 - side, axis=0), bit


def reduce_to_owner(parts):
    n = lax.axis_size("et")
    keep, give, bit = halve_over_et(parts)
    got = lax.ppermute(give, "et", [(i, i ^ bit) for i in range(n)])
    return keep.astype(jnp.float32) + got.astype(jnp.float32)


def reduce_to_previous(parts):
    n = lax.axis_size("et")
    stages = lax.axis_size("pipe")
    keep, give, bit = halve_over_et(parts)
    to_same = [(stage * n + i, (stage - 1) * n + i) for stage in range(1, stages) for i in range(n)]
    to_other = [(stage * n + i, (stage - 1) * n + (i ^ bit)) for stage in range(1, stages) for i in range(n)]
    first = lax.ppermute(keep, ("pipe", "et"), to_same)
    second = lax.ppermute(give, ("pipe", "et"), to_other)
    return first.astype(jnp.float32) + second.astype(jnp.float32)


def unpack(slot_sums, select):
    return lax.dot_general(
        select.astype(jnp.float32),
        slot_sums,
        (((0,), (0,)), ((), ())),
        precision=lax.Precision.HIGHEST,
        preferred_element_type=jnp.float32,
    ).astype(jnp.bfloat16)


def per_device(tokens, gate_vals, expert_ids, grad_out, w_gate, w_up, w_down):
    local_rows = tokens[0]
    local_grads = grad_out[0]
    gate_mats = w_gate[0]
    up_mats = w_up[0]
    down_mats = w_down[0]
    n = lax.axis_size("et")
    width = local_rows.shape[1]
    select, weights = local_slots(expert_ids[0], gate_vals[0])
    next_routes = shifted(expert_ids[0], "pipe", -1)
    next_select = local_slots(next_routes, gate_vals[0])[0]
    weight_cols = jnp.broadcast_to(weights.astype(jnp.bfloat16)[:, None], (E_WIN * MOST, TAIL))
    packed = jnp.concatenate(
        [pick_rows(select, local_rows), pick_rows(select, local_grads), weight_cols], axis=1
    )
    gathered = lax.all_gather(packed, "et", axis=0, tiled=True).reshape(n, E_WIN, MOST, 2 * width + TAIL)
    outs = []
    stored = []
    for expert in range(E_WIN):
        rows = gathered[:, expert, :, :width].reshape(n * MOST, width)
        gate_w = gathered[:, expert, :, 2 * width].reshape(n * MOST, 1).astype(jnp.float32)
        pre_gate = jnp.dot(rows, gate_mats[expert], preferred_element_type=jnp.float32)
        pre_up = jnp.dot(rows, up_mats[expert], preferred_element_type=jnp.float32)
        activated, slopes = silu_parts(pre_gate)
        hidden = (activated * pre_up).astype(jnp.bfloat16)
        out_e = gate_w * jnp.dot(hidden, down_mats[expert], preferred_element_type=jnp.float32)
        outs.append(out_e.astype(jnp.bfloat16).reshape(n, MOST, width))
        stored.append((gate_w, pre_up, activated, slopes))
    out_parts = jnp.stack(outs, axis=1).reshape(n, E_WIN * MOST, width)
    out_sums = reduce_to_owner(out_parts)
    grad_outs = []
    for expert in range(E_WIN):
        gate_w, pre_up, activated, slopes = stored[expert]
        grad_rows = gathered[:, expert, :, width : 2 * width].reshape(n * MOST, width)
        d_hidden = gate_w * lax.dot_general(
            grad_rows, down_mats[expert], (((1,), (1,)), ((), ())), preferred_element_type=jnp.float32
        )
        d_gate = (d_hidden * pre_up * slopes).astype(jnp.bfloat16)
        d_up = (d_hidden * activated).astype(jnp.bfloat16)
        grad_e = lax.dot_general(
            d_gate, gate_mats[expert], (((1,), (1,)), ((), ())), preferred_element_type=jnp.float32
        ) + lax.dot_general(d_up, up_mats[expert], (((1,), (1,)), ((), ())), preferred_element_type=jnp.float32)
        grad_outs.append(grad_e.astype(jnp.bfloat16).reshape(n, MOST, width))
    grad_parts = jnp.stack(grad_outs, axis=1).reshape(n, E_WIN * MOST, width)
    out_sums, grad_parts = lax.optimization_barrier((out_sums, grad_parts))
    received = unpack(reduce_to_previous(grad_parts), next_select)
    out_share = unpack(out_sums, select)
    return (out_share[None], received[None])


def solution(mesh):
    placed = (
        P("pipe", "et", None),
        P("pipe", "et", None),
        P("pipe", "et", None),
        P("pipe", "et", None),
        P("pipe", None, None, "et"),
        P("pipe", None, None, "et"),
        P("pipe", None, "et", None),
    )
    return jax.shard_map(
        per_device,
        mesh=mesh,
        in_specs=placed,
        out_specs=(P("pipe", "et", None), P("pipe", "et", None)),
        check_vma=False,
    )
```

```python
import jax
import jax.numpy as jnp
from jax import lax
from jax.experimental import pallas as pl
from jax.experimental.pallas import tpu as pltpu
from jax.sharding import PartitionSpec as P

E_WIN = 2
MOST = 16
TAIL = 128


def shifted(value, axis, steps):
    count = lax.axis_size(axis)
    first, last = (max(0, -steps), min(count, count - steps))
    return lax.ppermute(value, axis, [(source, source + steps) for source in range(first, last)])


def silu_parts(pre_gate):
    sigma = jax.nn.sigmoid(pre_gate)
    return (pre_gate * sigma, sigma * (1.0 + pre_gate * (1.0 - sigma)))


def local_slots(local_routes, local_gates):
    slot_ids = jnp.arange(MOST, dtype=jnp.int32)[:, None]
    selects, weights = [], []
    for expert in range(E_WIN):
        matches = local_routes == expert
        routed = jnp.any(matches, axis=1)
        gate_val = jnp.sum(jnp.where(matches, local_gates.astype(jnp.float32), 0.0), axis=1)
        positions = jnp.cumsum(routed.astype(jnp.int32), dtype=jnp.int32) - 1
        select = routed[None, :] & (positions[None, :] == slot_ids)
        selects.append(select)
        weights.append(jnp.sum(jnp.where(select, gate_val[None, :], 0.0), axis=1))
    return jnp.concatenate(selects, axis=0), jnp.concatenate(weights)


def pick_rows(select, rows):
    return jnp.dot(select.astype(rows.dtype), rows, preferred_element_type=jnp.float32).astype(rows.dtype)


def halve_over_et(parts):
    n = lax.axis_size("et")
    me = lax.axis_index("et")
    held = parts
    bit = 1
    while 2 * bit < n:
        halves = held.reshape((held.shape[0] // 2, 2) + held.shape[1:])
        side = (me // bit) % 2
        keep = jnp.take(halves, side, axis=1)
        give = jnp.take(halves, 1 - side, axis=1)
        got = lax.ppermute(give, "et", [(i, i ^ bit) for i in range(n)])
        held = (keep.astype(jnp.float32) + got.astype(jnp.float32)).astype(jnp.bfloat16)
        bit *= 2
    side = (me // bit) % 2
    return jnp.take(held, side, axis=0), jnp.take(held, 1 - side, axis=0), bit


def reduce_to_owner(parts):
    n = lax.axis_size("et")
    keep, give, bit = halve_over_et(parts)
    got = lax.ppermute(give, "et", [(i, i ^ bit) for i in range(n)])
    return keep.astype(jnp.float32) + got.astype(jnp.float32)


def reduce_to_previous(parts):
    n = lax.axis_size("et")
    stages = lax.axis_size("pipe")
    keep, give, bit = halve_over_et(parts)
    to_same = [(stage * n + i, (stage - 1) * n + i) for stage in range(1, stages) for i in range(n)]
    to_other = [(stage * n + i, (stage - 1) * n + (i ^ bit)) for stage in range(1, stages) for i in range(n)]
    first = lax.ppermute(keep, ("pipe", "et"), to_same)
    second = lax.ppermute(give, ("pipe", "et"), to_other)
    return first.astype(jnp.float32) + second.astype(jnp.float32)


def unpack(slot_sums, select):
    return lax.dot_general(
        select.astype(jnp.float32),
        slot_sums,
        (((0,), (0,)), ((), ())),
        precision=lax.Precision.HIGHEST,
        preferred_element_type=jnp.float32,
    ).astype(jnp.bfloat16)


def _expert_body(x_ref, g_ref, w_ref, wg_ref, wu_ref, wd_ref, out_ref, grad_ref, out_acc, grad_acc):
    step = pl.program_id(1)
    rows = x_ref.shape[0] * x_ref.shape[1]
    width = x_ref.shape[2]

    @pl.when(step == 0)
    def _():
        out_acc[...] = jnp.zeros_like(out_acc)
        grad_acc[...] = jnp.zeros_like(grad_acc)

    x = x_ref[...].reshape(rows, width)
    g = g_ref[...].reshape(rows, width)
    gate_w = w_ref[...].reshape(rows, w_ref.shape[2])[:, 0:1].astype(jnp.float32)
    wg = wg_ref[...]
    wu = wu_ref[...]
    wd = wd_ref[...]
    pre_gate = jnp.dot(x, wg, preferred_element_type=jnp.float32)
    pre_up = jnp.dot(x, wu, preferred_element_type=jnp.float32)
    d_hidden = gate_w * lax.dot_general(g, wd, (((1,), (1,)), ((), ())), preferred_element_type=jnp.float32)
    sigma = jax.nn.sigmoid(pre_gate)
    activated = pre_gate * sigma
    slopes = sigma * (1.0 + pre_gate * (1.0 - sigma))
    hidden = (activated * pre_up).astype(jnp.bfloat16)
    out_acc[...] += jnp.dot(hidden, wd, preferred_element_type=jnp.float32)
    d_gate = (d_hidden * pre_up * slopes).astype(jnp.bfloat16)
    d_up = (d_hidden * activated).astype(jnp.bfloat16)
    grad_acc[...] += lax.dot_general(
        d_gate, wg, (((1,), (1,)), ((), ())), preferred_element_type=jnp.float32
    ) + lax.dot_general(d_up, wu, (((1,), (1,)), ((), ())), preferred_element_type=jnp.float32)

    @pl.when(step == pl.num_programs(1) - 1)
    def _():
        out_ref[...] = (gate_w * out_acc[...]).astype(out_ref.dtype).reshape(out_ref.shape)
        grad_ref[...] = grad_acc[...].astype(grad_ref.dtype).reshape(grad_ref.shape)


def expert_pass(gathered, gate_mats, up_mats, down_mats):
    n, experts, most, packed_width = gathered.shape
    width = gate_mats.shape[1]
    shard = gate_mats.shape[2]
    tile = 128 if shard % 128 == 0 else shard
    steps = shard // tile
    rows = n * most
    return pl.pallas_call(
        _expert_body,
        grid=(experts, steps),
        in_specs=[
            pl.BlockSpec((n, None, most, width), lambda e, f: (0, e, 0, 0)),
            pl.BlockSpec((n, None, most, width), lambda e, f: (0, e, 0, 1)),
            pl.BlockSpec((n, None, most, TAIL), lambda e, f: (0, e, 0, 2 * width // TAIL)),
            pl.BlockSpec((None, width, tile), lambda e, f: (e, 0, f)),
            pl.BlockSpec((None, width, tile), lambda e, f: (e, 0, f)),
            pl.BlockSpec((None, tile, width), lambda e, f: (e, f, 0)),
        ],
        out_specs=[
            pl.BlockSpec((n, None, most, width), lambda e, f: (0, e, 0, 0)),
            pl.BlockSpec((n, None, most, width), lambda e, f: (0, e, 0, 0)),
        ],
        out_shape=[
            jax.ShapeDtypeStruct((n, experts, most, width), jnp.bfloat16),
            jax.ShapeDtypeStruct((n, experts, most, width), jnp.bfloat16),
        ],
        scratch_shapes=[pltpu.VMEM((rows, width), jnp.float32), pltpu.VMEM((rows, width), jnp.float32)],
        compiler_params=pltpu.CompilerParams(
            dimension_semantics=("arbitrary", "arbitrary"), vmem_limit_bytes=100 * 1024 * 1024
        ),
    )(gathered, gathered, gathered, gate_mats, up_mats, down_mats)


def per_device(tokens, gate_vals, expert_ids, grad_out, w_gate, w_up, w_down):
    local_rows = tokens[0]
    local_grads = grad_out[0]
    gate_mats = w_gate[0]
    up_mats = w_up[0]
    down_mats = w_down[0]
    n = lax.axis_size("et")
    width = local_rows.shape[1]
    select, weights = local_slots(expert_ids[0], gate_vals[0])
    next_routes = shifted(expert_ids[0], "pipe", -1)
    next_select = local_slots(next_routes, gate_vals[0])[0]
    weight_cols = jnp.broadcast_to(weights.astype(jnp.bfloat16)[:, None], (E_WIN * MOST, TAIL))
    packed = jnp.concatenate(
        [pick_rows(select, local_rows), pick_rows(select, local_grads), weight_cols], axis=1
    )
    gathered = lax.all_gather(packed, "et", axis=0, tiled=True).reshape(n, E_WIN, MOST, 2 * width + TAIL)
    out_parts, grad_parts = expert_pass(gathered, gate_mats, up_mats, down_mats)
    out_sums = reduce_to_owner(out_parts.reshape(n, E_WIN * MOST, width))
    received = unpack(reduce_to_previous(grad_parts.reshape(n, E_WIN * MOST, width)), next_select)
    out_share = unpack(out_sums, select)
    return (out_share[None], received[None])


def solution(mesh):
    placed = (
        P("pipe", "et", None),
        P("pipe", "et", None),
        P("pipe", "et", None),
        P("pipe", "et", None),
        P("pipe", None, None, "et"),
        P("pipe", None, None, "et"),
        P("pipe", None, "et", None),
    )
    return jax.shard_map(
        per_device,
        mesh=mesh,
        in_specs=placed,
        out_specs=(P("pipe", "et", None), P("pipe", "et", None)),
        check_vma=False,
    )
```

```python
import jax
import jax.numpy as jnp
from jax import lax
from jax.experimental import pallas as pl
from jax.experimental.pallas import tpu as pltpu
from jax.sharding import PartitionSpec as P

E_WIN = 2
MOST = 16
TAIL = 128


def shifted(value, axis, steps):
    count = lax.axis_size(axis)
    first, last = (max(0, -steps), min(count, count - steps))
    return lax.ppermute(value, axis, [(source, source + steps) for source in range(first, last)])


def silu_parts(pre_gate):
    sigma = jax.nn.sigmoid(pre_gate)
    return (pre_gate * sigma, sigma * (1.0 + pre_gate * (1.0 - sigma)))


def local_slots(local_routes, local_gates):
    slot_ids = jnp.arange(MOST, dtype=jnp.int32)[:, None]
    selects, weights = [], []
    for expert in range(E_WIN):
        matches = local_routes == expert
        routed = jnp.any(matches, axis=1)
        gate_val = jnp.sum(jnp.where(matches, local_gates.astype(jnp.float32), 0.0), axis=1)
        positions = jnp.cumsum(routed.astype(jnp.int32), dtype=jnp.int32) - 1
        select = routed[None, :] & (positions[None, :] == slot_ids)
        selects.append(select)
        weights.append(jnp.sum(jnp.where(select, gate_val[None, :], 0.0), axis=1))
    return jnp.concatenate(selects, axis=0), jnp.concatenate(weights)


def pick_rows(select, rows):
    return jnp.dot(select.astype(rows.dtype), rows, preferred_element_type=jnp.float32).astype(rows.dtype)


def halve_over_et(parts, order, hook):
    n = lax.axis_size("et")
    me = lax.axis_index("et")
    remaining = sorted(order)
    held = parts
    for bit in order[:-1]:
        lower = 1 << remaining.index(bit)
        count = held.shape[0]
        halves = held.reshape((count // (2 * lower), 2, lower) + held.shape[1:])
        side = (me // bit) % 2
        keep = jnp.take(halves, side, axis=1).reshape((count // 2,) + held.shape[1:])
        give = jnp.take(halves, 1 - side, axis=1).reshape((count // 2,) + held.shape[1:])
        got = lax.ppermute(give, "et", [(i, i ^ bit) for i in range(n)])
        held = (keep.astype(jnp.float32) + got.astype(jnp.float32)).astype(jnp.bfloat16)
        held = hook(held)
        hook = lambda value: value
        remaining.remove(bit)
    bit = order[-1]
    side = (me // bit) % 2
    return jnp.take(held, side, axis=0), jnp.take(held, 1 - side, axis=0), bit


def round_order(n, early):
    bits = [1 << k for k in range(n.bit_length() - 1)]
    head = bits[:-1]
    if early in head:
        head = [early] + [bit for bit in head if bit != early]
    return head + bits[-1:]


def reduce_to_owner(parts, order, hook):
    n = lax.axis_size("et")
    keep, give, bit = halve_over_et(parts, order, hook)
    got = lax.ppermute(give, "et", [(i, i ^ bit) for i in range(n)])
    return keep.astype(jnp.float32) + got.astype(jnp.float32)


def reduce_to_previous(parts, order, hook):
    n = lax.axis_size("et")
    stages = lax.axis_size("pipe")
    keep, give, bit = halve_over_et(parts, order, hook)
    to_same = [(stage * n + i, (stage - 1) * n + i) for stage in range(1, stages) for i in range(n)]
    to_other = [(stage * n + i, (stage - 1) * n + (i ^ bit)) for stage in range(1, stages) for i in range(n)]
    first = lax.ppermute(keep, ("pipe", "et"), to_same)
    second = lax.ppermute(give, ("pipe", "et"), to_other)
    return first.astype(jnp.float32) + second.astype(jnp.float32)


def unpack(slot_sums, select):
    return lax.dot_general(
        select.astype(jnp.float32),
        slot_sums,
        (((0,), (0,)), ((), ())),
        precision=lax.Precision.HIGHEST,
        preferred_element_type=jnp.float32,
    ).astype(jnp.bfloat16)


def _expert_body(x_ref, g_ref, w_ref, wg_ref, wu_ref, wd_ref, out_ref, grad_ref, out_acc, grad_acc):
    step = pl.program_id(1)
    rows = x_ref.shape[0] * x_ref.shape[1]
    width = x_ref.shape[2]

    @pl.when(step == 0)
    def _():
        out_acc[...] = jnp.zeros_like(out_acc)
        grad_acc[...] = jnp.zeros_like(grad_acc)

    x = x_ref[...].reshape(rows, width)
    g = g_ref[...].reshape(rows, width)
    gate_w = w_ref[...].reshape(rows, w_ref.shape[2])[:, 0:1].astype(jnp.float32)
    wg = wg_ref[...]
    wu = wu_ref[...]
    wd = wd_ref[...]
    pre_gate = jnp.dot(x, wg, preferred_element_type=jnp.float32)
    pre_up = jnp.dot(x, wu, preferred_element_type=jnp.float32)
    d_hidden = gate_w * lax.dot_general(g, wd, (((1,), (1,)), ((), ())), preferred_element_type=jnp.float32)
    sigma = jax.nn.sigmoid(pre_gate)
    activated = pre_gate * sigma
    slopes = sigma * (1.0 + pre_gate * (1.0 - sigma))
    hidden = (activated * pre_up).astype(jnp.bfloat16)
    out_acc[...] += jnp.dot(hidden, wd, preferred_element_type=jnp.float32)
    d_gate = (d_hidden * pre_up * slopes).astype(jnp.bfloat16)
    d_up = (d_hidden * activated).astype(jnp.bfloat16)
    grad_acc[...] += lax.dot_general(
        d_gate, wg, (((1,), (1,)), ((), ())), preferred_element_type=jnp.float32
    ) + lax.dot_general(d_up, wu, (((1,), (1,)), ((), ())), preferred_element_type=jnp.float32)

    @pl.when(step == pl.num_programs(1) - 1)
    def _():
        out_ref[...] = (gate_w * out_acc[...]).astype(out_ref.dtype).reshape(out_ref.shape)
        grad_ref[...] = grad_acc[...].astype(grad_ref.dtype).reshape(grad_ref.shape)


def expert_pass(gathered, gate_mats, up_mats, down_mats, expert):
    n, experts, most, packed_width = gathered.shape
    width = gate_mats.shape[1]
    shard = gate_mats.shape[2]
    tile = 128 if shard % 128 == 0 else shard
    steps = shard // tile
    rows = n * most
    return pl.pallas_call(
        _expert_body,
        grid=(1, steps),
        in_specs=[
            pl.BlockSpec((n, None, most, width), lambda e, f: (0, expert, 0, 0)),
            pl.BlockSpec((n, None, most, width), lambda e, f: (0, expert, 0, 1)),
            pl.BlockSpec((n, None, most, TAIL), lambda e, f: (0, expert, 0, 2 * width // TAIL)),
            pl.BlockSpec((None, width, tile), lambda e, f: (expert, 0, f)),
            pl.BlockSpec((None, width, tile), lambda e, f: (expert, 0, f)),
            pl.BlockSpec((None, tile, width), lambda e, f: (expert, f, 0)),
        ],
        out_specs=[
            pl.BlockSpec((n, most, width), lambda e, f: (0, 0, 0)),
            pl.BlockSpec((n, most, width), lambda e, f: (0, 0, 0)),
        ],
        out_shape=[
            jax.ShapeDtypeStruct((n, most, width), jnp.bfloat16),
            jax.ShapeDtypeStruct((n, most, width), jnp.bfloat16),
        ],
        scratch_shapes=[pltpu.VMEM((rows, width), jnp.float32), pltpu.VMEM((rows, width), jnp.float32)],
        compiler_params=pltpu.CompilerParams(
            dimension_semantics=("arbitrary", "arbitrary"), vmem_limit_bytes=100 * 1024 * 1024
        ),
        cost_estimate=pl.CostEstimate(
            flops=12 * rows * width * shard,
            transcendentals=rows * shard,
            bytes_accessed=6 * width * shard + 8 * rows * width,
        ),
    )(gathered, gathered, gathered, gate_mats, up_mats, down_mats)


def per_device(tokens, gate_vals, expert_ids, grad_out, w_gate, w_up, w_down):
    local_rows = tokens[0]
    local_grads = grad_out[0]
    gate_mats = w_gate[0]
    up_mats = w_up[0]
    down_mats = w_down[0]
    n = lax.axis_size("et")
    width = local_rows.shape[1]
    select, weights = local_slots(expert_ids[0], gate_vals[0])
    next_routes = shifted(expert_ids[0], "pipe", -1)
    next_select = local_slots(next_routes, gate_vals[0])[0]
    weight_cols = jnp.broadcast_to(weights.astype(jnp.bfloat16)[:, None], (E_WIN * MOST, TAIL))
    packed = jnp.concatenate(
        [pick_rows(select, local_rows), pick_rows(select, local_grads), weight_cols], axis=1
    )
    gathered = lax.all_gather(packed, "et", axis=0, tiled=True).reshape(n, E_WIN, MOST, 2 * width + TAIL)
    out_sums, grad_sums = [], []
    same = lambda value: value
    for expert in range(E_WIN):
        out_part, grad_part = expert_pass(gathered, gate_mats, up_mats, down_mats, expert)
        if out_sums:
            out_sums, grad_sums, out_part, grad_part = lax.optimization_barrier(
                (out_sums, grad_sums, out_part, grad_part)
            )
        order = round_order(n, 2 if expert + 1 < E_WIN else 1)
        out_sums.append(reduce_to_owner(out_part, order, same))
        grad_sums.append(reduce_to_previous(grad_part, order, same))
    out_share = unpack(jnp.concatenate(out_sums, axis=0), select)
    received = unpack(jnp.concatenate(grad_sums, axis=0), next_select)
    return (out_share[None], received[None])


def solution(mesh):
    placed = (
        P("pipe", "et", None),
        P("pipe", "et", None),
        P("pipe", "et", None),
        P("pipe", "et", None),
        P("pipe", None, None, "et"),
        P("pipe", None, None, "et"),
        P("pipe", None, "et", None),
    )
    return jax.shard_map(
        per_device,
        mesh=mesh,
        in_specs=placed,
        out_specs=(P("pipe", "et", None), P("pipe", "et", None)),
        check_vma=False,
    )
```

```python
import jax
import jax.numpy as jnp
from jax import lax
from jax.experimental import pallas as pl
from jax.experimental.pallas import tpu as pltpu
from jax.sharding import PartitionSpec as P

E_WIN = 2
MOST = 16
TAIL = 128


def shifted(value, axis, steps):
    count = lax.axis_size(axis)
    first, last = (max(0, -steps), min(count, count - steps))
    return lax.ppermute(value, axis, [(source, source + steps) for source in range(first, last)])


def silu_parts(pre_gate):
    sigma = jax.nn.sigmoid(pre_gate)
    return (pre_gate * sigma, sigma * (1.0 + pre_gate * (1.0 - sigma)))


def local_slots(local_routes, local_gates):
    slot_ids = jnp.arange(MOST, dtype=jnp.int32)[:, None]
    selects, weights = [], []
    for expert in range(E_WIN):
        matches = local_routes == expert
        routed = jnp.any(matches, axis=1)
        gate_val = jnp.sum(jnp.where(matches, local_gates.astype(jnp.float32), 0.0), axis=1)
        positions = jnp.cumsum(routed.astype(jnp.int32), dtype=jnp.int32) - 1
        select = routed[None, :] & (positions[None, :] == slot_ids)
        selects.append(select)
        weights.append(jnp.sum(jnp.where(select, gate_val[None, :], 0.0), axis=1))
    return jnp.concatenate(selects, axis=0), jnp.concatenate(weights)


def pick_rows(select, rows):
    return jnp.dot(select.astype(rows.dtype), rows, preferred_element_type=jnp.float32).astype(rows.dtype)


def gather_over_et(packed):
    n = lax.axis_size("et")
    held = packed[None]
    bit = 1
    while bit < n:
        got = lax.ppermute(held, "et", [(i, i ^ bit) for i in range(n)])
        held = jnp.concatenate([held, got], axis=0)
        bit *= 2
    return held


def halve_over_et(parts):
    n = lax.axis_size("et")
    held = parts
    bit = 1
    while 2 * bit < n:
        halves = held.reshape((held.shape[0] // 2, 2) + held.shape[1:])
        got = lax.ppermute(halves[:, 1], "et", [(i, i ^ bit) for i in range(n)])
        held = (halves[:, 0].astype(jnp.float32) + got.astype(jnp.float32)).astype(jnp.bfloat16)
        bit *= 2
    return held[0], held[1], bit


def reduce_to_owner(parts):
    n = lax.axis_size("et")
    keep, give, bit = halve_over_et(parts)
    got = lax.ppermute(give, "et", [(i, i ^ bit) for i in range(n)])
    return keep.astype(jnp.float32) + got.astype(jnp.float32)


def reduce_to_previous(parts):
    n = lax.axis_size("et")
    stages = lax.axis_size("pipe")
    keep, give, bit = halve_over_et(parts)
    to_same = [(stage * n + i, (stage - 1) * n + i) for stage in range(1, stages) for i in range(n)]
    to_other = [(stage * n + i, (stage - 1) * n + (i ^ bit)) for stage in range(1, stages) for i in range(n)]
    first = lax.ppermute(keep, ("pipe", "et"), to_same)
    second = lax.ppermute(give, ("pipe", "et"), to_other)
    return first.astype(jnp.float32) + second.astype(jnp.float32)


def unpack(slot_sums, select):
    return lax.dot_general(
        select.astype(jnp.float32),
        slot_sums,
        (((0,), (0,)), ((), ())),
        precision=lax.Precision.HIGHEST,
        preferred_element_type=jnp.float32,
    ).astype(jnp.bfloat16)


def _expert_body(x_ref, g_ref, w_ref, wg_ref, wu_ref, wd_ref, out_ref, grad_ref, out_acc, grad_acc):
    step = pl.program_id(1)
    rows = x_ref.shape[0] * x_ref.shape[1]
    width = x_ref.shape[2]

    @pl.when(step == 0)
    def _():
        out_acc[...] = jnp.zeros_like(out_acc)
        grad_acc[...] = jnp.zeros_like(grad_acc)

    x = x_ref[...].reshape(rows, width)
    g = g_ref[...].reshape(rows, width)
    gate_w = w_ref[...].reshape(rows, w_ref.shape[2])[:, 0:1].astype(jnp.float32)
    wg = wg_ref[...]
    wu = wu_ref[...]
    wd = wd_ref[...]
    pre_gate = jnp.dot(x, wg, preferred_element_type=jnp.float32)
    pre_up = jnp.dot(x, wu, preferred_element_type=jnp.float32)
    d_hidden = gate_w * lax.dot_general(g, wd, (((1,), (1,)), ((), ())), preferred_element_type=jnp.float32)
    sigma = jax.nn.sigmoid(pre_gate)
    activated = pre_gate * sigma
    slopes = sigma * (1.0 + pre_gate * (1.0 - sigma))
    hidden = (activated * pre_up).astype(jnp.bfloat16)
    out_acc[...] += jnp.dot(hidden, wd, preferred_element_type=jnp.float32)
    d_gate = (d_hidden * pre_up * slopes).astype(jnp.bfloat16)
    d_up = (d_hidden * activated).astype(jnp.bfloat16)
    grad_acc[...] += lax.dot_general(
        d_gate, wg, (((1,), (1,)), ((), ())), preferred_element_type=jnp.float32
    ) + lax.dot_general(d_up, wu, (((1,), (1,)), ((), ())), preferred_element_type=jnp.float32)

    @pl.when(step == pl.num_programs(1) - 1)
    def _():
        out_ref[...] = (gate_w * out_acc[...]).astype(out_ref.dtype).reshape(out_ref.shape)
        grad_ref[...] = grad_acc[...].astype(grad_ref.dtype).reshape(grad_ref.shape)


def expert_pass(gathered, gate_mats, up_mats, down_mats):
    n, experts, most, packed_width = gathered.shape
    width = gate_mats.shape[1]
    shard = gate_mats.shape[2]
    tile = 128 if shard % 128 == 0 else shard
    steps = shard // tile
    rows = n * most
    return pl.pallas_call(
        _expert_body,
        grid=(experts, steps),
        in_specs=[
            pl.BlockSpec((n, None, most, width), lambda e, f: (0, e, 0, 0)),
            pl.BlockSpec((n, None, most, width), lambda e, f: (0, e, 0, 1)),
            pl.BlockSpec((n, None, most, TAIL), lambda e, f: (0, e, 0, 2 * width // TAIL)),
            pl.BlockSpec((None, width, tile), lambda e, f: (e, 0, f)),
            pl.BlockSpec((None, width, tile), lambda e, f: (e, 0, f)),
            pl.BlockSpec((None, tile, width), lambda e, f: (e, f, 0)),
        ],
        out_specs=[
            pl.BlockSpec((n, None, most, width), lambda e, f: (0, e, 0, 0)),
            pl.BlockSpec((n, None, most, width), lambda e, f: (0, e, 0, 0)),
        ],
        out_shape=[
            jax.ShapeDtypeStruct((n, experts, most, width), jnp.bfloat16),
            jax.ShapeDtypeStruct((n, experts, most, width), jnp.bfloat16),
        ],
        scratch_shapes=[pltpu.VMEM((rows, width), jnp.float32), pltpu.VMEM((rows, width), jnp.float32)],
        compiler_params=pltpu.CompilerParams(
            dimension_semantics=("arbitrary", "arbitrary"), vmem_limit_bytes=100 * 1024 * 1024
        ),
    )(gathered, gathered, gathered, gate_mats, up_mats, down_mats)


def per_device(tokens, gate_vals, expert_ids, grad_out, w_gate, w_up, w_down):
    local_rows = tokens[0]
    local_grads = grad_out[0]
    gate_mats = w_gate[0]
    up_mats = w_up[0]
    down_mats = w_down[0]
    n = lax.axis_size("et")
    width = local_rows.shape[1]
    select, weights = local_slots(expert_ids[0], gate_vals[0])
    next_routes = shifted(expert_ids[0], "pipe", -1)
    next_select = local_slots(next_routes, gate_vals[0])[0]
    weight_cols = jnp.broadcast_to(weights.astype(jnp.bfloat16)[:, None], (E_WIN * MOST, TAIL))
    packed = jnp.concatenate(
        [pick_rows(select, local_rows), pick_rows(select, local_grads), weight_cols], axis=1
    )
    gathered = gather_over_et(packed).reshape(n, E_WIN, MOST, 2 * width + TAIL)
    out_parts, grad_parts = expert_pass(gathered, gate_mats, up_mats, down_mats)
    out_sums = reduce_to_owner(out_parts.reshape(n, E_WIN * MOST, width))
    received = unpack(reduce_to_previous(grad_parts.reshape(n, E_WIN * MOST, width)), next_select)
    out_share = unpack(out_sums, select)
    return (out_share[None], received[None])


def solution(mesh):
    placed = (
        P("pipe", "et", None),
        P("pipe", "et", None),
        P("pipe", "et", None),
        P("pipe", "et", None),
        P("pipe", None, None, "et"),
        P("pipe", None, None, "et"),
        P("pipe", None, "et", None),
    )
    return jax.shard_map(
        per_device,
        mesh=mesh,
        in_specs=placed,
        out_specs=(P("pipe", "et", None), P("pipe", "et", None)),
        check_vma=False,
    )
```

```python
import jax
import jax.numpy as jnp
from jax import lax
from jax.experimental import pallas as pl
from jax.experimental.pallas import tpu as pltpu
from jax.sharding import PartitionSpec as P

E_WIN = 2
MOST = 16
TAIL = 128


def shifted(value, axis, steps):
    count = lax.axis_size(axis)
    first, last = (max(0, -steps), min(count, count - steps))
    return lax.ppermute(value, axis, [(source, source + steps) for source in range(first, last)])


def silu_parts(pre_gate):
    sigma = jax.nn.sigmoid(pre_gate)
    return (pre_gate * sigma, sigma * (1.0 + pre_gate * (1.0 - sigma)))


def local_slots(local_routes, local_gates):
    slot_ids = jnp.arange(MOST, dtype=jnp.int32)[:, None]
    selects, weights = [], []
    for expert in range(E_WIN):
        matches = local_routes == expert
        routed = jnp.any(matches, axis=1)
        gate_val = jnp.sum(jnp.where(matches, local_gates.astype(jnp.float32), 0.0), axis=1)
        positions = jnp.cumsum(routed.astype(jnp.int32), dtype=jnp.int32) - 1
        select = routed[None, :] & (positions[None, :] == slot_ids)
        selects.append(select)
        weights.append(jnp.sum(jnp.where(select, gate_val[None, :], 0.0), axis=1))
    return jnp.concatenate(selects, axis=0), jnp.concatenate(weights)


def pick_rows(select, rows):
    return jnp.dot(select.astype(rows.dtype), rows, preferred_element_type=jnp.float32).astype(rows.dtype)


def halve_over_et(parts, order, hook):
    n = lax.axis_size("et")
    me = lax.axis_index("et")
    remaining = sorted(order)
    held = parts
    for bit in order[:-1]:
        lower = 1 << remaining.index(bit)
        count = held.shape[0]
        halves = held.reshape((count // (2 * lower), 2, lower) + held.shape[1:])
        side = (me // bit) % 2
        keep = jnp.take(halves, side, axis=1).reshape((count // 2,) + held.shape[1:])
        give = jnp.take(halves, 1 - side, axis=1).reshape((count // 2,) + held.shape[1:])
        got = lax.ppermute(give, "et", [(i, i ^ bit) for i in range(n)])
        held = (keep.astype(jnp.float32) + got.astype(jnp.float32)).astype(jnp.bfloat16)
        held = hook(held)
        hook = lambda value: value
        remaining.remove(bit)
    bit = order[-1]
    side = (me // bit) % 2
    return jnp.take(held, side, axis=0), jnp.take(held, 1 - side, axis=0), bit


def round_order(n, late):
    bits = [1 << k for k in range(n.bit_length() - 1)]
    if late in bits:
        bits = [bit for bit in bits if bit != late] + [late]
    return bits


def reduce_to_owner(parts, order, hook):
    n = lax.axis_size("et")
    keep, give, bit = halve_over_et(parts, order, hook)
    got = lax.ppermute(give, "et", [(i, i ^ bit) for i in range(n)])
    return keep.astype(jnp.float32) + got.astype(jnp.float32)


def reduce_to_previous(parts, order, hook):
    n = lax.axis_size("et")
    stages = lax.axis_size("pipe")
    keep, give, bit = halve_over_et(parts, order, hook)
    to_same = [(stage * n + i, (stage - 1) * n + i) for stage in range(1, stages) for i in range(n)]
    to_other = [(stage * n + i, (stage - 1) * n + (i ^ bit)) for stage in range(1, stages) for i in range(n)]
    first = lax.ppermute(keep, ("pipe", "et"), to_same)
    second = lax.ppermute(give, ("pipe", "et"), to_other)
    return first.astype(jnp.float32) + second.astype(jnp.float32)


def unpack(slot_sums, select):
    return lax.dot_general(
        select.astype(jnp.float32),
        slot_sums,
        (((0,), (0,)), ((), ())),
        precision=lax.Precision.HIGHEST,
        preferred_element_type=jnp.float32,
    ).astype(jnp.bfloat16)


def _expert_body(x_ref, g_ref, w_ref, wg_ref, wu_ref, wd_ref, out_ref, grad_ref, out_acc, grad_acc):
    step = pl.program_id(1)
    rows = x_ref.shape[0] * x_ref.shape[1]
    width = x_ref.shape[2]

    @pl.when(step == 0)
    def _():
        out_acc[...] = jnp.zeros_like(out_acc)
        grad_acc[...] = jnp.zeros_like(grad_acc)

    x = x_ref[...].reshape(rows, width)
    g = g_ref[...].reshape(rows, width)
    gate_w = w_ref[...].reshape(rows, w_ref.shape[2])[:, 0:1].astype(jnp.float32)
    wg = wg_ref[...]
    wu = wu_ref[...]
    wd = wd_ref[...]
    pre_gate = jnp.dot(x, wg, preferred_element_type=jnp.float32)
    pre_up = jnp.dot(x, wu, preferred_element_type=jnp.float32)
    d_hidden = gate_w * lax.dot_general(g, wd, (((1,), (1,)), ((), ())), preferred_element_type=jnp.float32)
    sigma = jax.nn.sigmoid(pre_gate)
    activated = pre_gate * sigma
    slopes = sigma * (1.0 + pre_gate * (1.0 - sigma))
    hidden = (activated * pre_up).astype(jnp.bfloat16)
    out_acc[...] += jnp.dot(hidden, wd, preferred_element_type=jnp.float32)
    d_gate = (d_hidden * pre_up * slopes).astype(jnp.bfloat16)
    d_up = (d_hidden * activated).astype(jnp.bfloat16)
    grad_acc[...] += lax.dot_general(
        d_gate, wg, (((1,), (1,)), ((), ())), preferred_element_type=jnp.float32
    ) + lax.dot_general(d_up, wu, (((1,), (1,)), ((), ())), preferred_element_type=jnp.float32)

    @pl.when(step == pl.num_programs(1) - 1)
    def _():
        out_ref[...] = (gate_w * out_acc[...]).astype(out_ref.dtype).reshape(out_ref.shape)
        grad_ref[...] = grad_acc[...].astype(grad_ref.dtype).reshape(grad_ref.shape)


def expert_pass(gathered, gate_mats, up_mats, down_mats):
    n, experts, most, packed_width = gathered.shape
    width = gate_mats.shape[1]
    shard = gate_mats.shape[2]
    tile = 128 if shard % 128 == 0 else shard
    steps = shard // tile
    rows = n * most
    return pl.pallas_call(
        _expert_body,
        grid=(experts, steps),
        in_specs=[
            pl.BlockSpec((n, None, most, width), lambda e, f: (0, e, 0, 0)),
            pl.BlockSpec((n, None, most, width), lambda e, f: (0, e, 0, 1)),
            pl.BlockSpec((n, None, most, TAIL), lambda e, f: (0, e, 0, 2 * width // TAIL)),
            pl.BlockSpec((None, width, tile), lambda e, f: (e, 0, f)),
            pl.BlockSpec((None, width, tile), lambda e, f: (e, 0, f)),
            pl.BlockSpec((None, tile, width), lambda e, f: (e, f, 0)),
        ],
        out_specs=[
            pl.BlockSpec((n, None, most, width), lambda e, f: (0, e, 0, 0)),
            pl.BlockSpec((n, None, most, width), lambda e, f: (0, e, 0, 0)),
        ],
        out_shape=[
            jax.ShapeDtypeStruct((n, experts, most, width), jnp.bfloat16),
            jax.ShapeDtypeStruct((n, experts, most, width), jnp.bfloat16),
        ],
        scratch_shapes=[pltpu.VMEM((rows, width), jnp.float32), pltpu.VMEM((rows, width), jnp.float32)],
        compiler_params=pltpu.CompilerParams(
            dimension_semantics=("arbitrary", "arbitrary"), vmem_limit_bytes=100 * 1024 * 1024
        ),
    )(gathered, gathered, gathered, gate_mats, up_mats, down_mats)


def per_device(tokens, gate_vals, expert_ids, grad_out, w_gate, w_up, w_down):
    local_rows = tokens[0]
    local_grads = grad_out[0]
    gate_mats = w_gate[0]
    up_mats = w_up[0]
    down_mats = w_down[0]
    n = lax.axis_size("et")
    width = local_rows.shape[1]
    select, weights = local_slots(expert_ids[0], gate_vals[0])
    next_routes = shifted(expert_ids[0], "pipe", -1)
    next_select = local_slots(next_routes, gate_vals[0])[0]
    weight_cols = jnp.broadcast_to(weights.astype(jnp.bfloat16)[:, None], (E_WIN * MOST, TAIL))
    packed = jnp.concatenate(
        [pick_rows(select, local_rows), pick_rows(select, local_grads), weight_cols], axis=1
    )
    gathered = lax.all_gather(packed, "et", axis=0, tiled=True).reshape(n, E_WIN, MOST, 2 * width + TAIL)
    out_parts, grad_parts = expert_pass(gathered, gate_mats, up_mats, down_mats)
    same = lambda value: value
    out_sums = reduce_to_owner(out_parts.reshape(n, E_WIN * MOST, width), round_order(n, n // 2), same)
    received = unpack(
        reduce_to_previous(grad_parts.reshape(n, E_WIN * MOST, width), round_order(n, 2), same), next_select
    )
    out_share = unpack(out_sums, select)
    return (out_share[None], received[None])


def solution(mesh):
    placed = (
        P("pipe", "et", None),
        P("pipe", "et", None),
        P("pipe", "et", None),
        P("pipe", "et", None),
        P("pipe", None, None, "et"),
        P("pipe", None, None, "et"),
        P("pipe", None, "et", None),
    )
    return jax.shard_map(
        per_device,
        mesh=mesh,
        in_specs=placed,
        out_specs=(P("pipe", "et", None), P("pipe", "et", None)),
        check_vma=False,
    )
```

```python
import jax
import jax.numpy as jnp
from jax import lax
from jax.experimental import pallas as pl
from jax.experimental.pallas import tpu as pltpu
from jax.sharding import PartitionSpec as P

E_WIN = 2
MOST = 16
TAIL = 128


def shifted(value, axis, steps):
    count = lax.axis_size(axis)
    first, last = (max(0, -steps), min(count, count - steps))
    return lax.ppermute(value, axis, [(source, source + steps) for source in range(first, last)])


def silu_parts(pre_gate):
    sigma = jax.nn.sigmoid(pre_gate)
    return (pre_gate * sigma, sigma * (1.0 + pre_gate * (1.0 - sigma)))


def local_slots(local_routes, local_gates):
    slot_ids = jnp.arange(MOST, dtype=jnp.int32)[:, None]
    selects, weights = [], []
    for expert in range(E_WIN):
        matches = local_routes == expert
        routed = jnp.any(matches, axis=1)
        gate_val = jnp.sum(jnp.where(matches, local_gates.astype(jnp.float32), 0.0), axis=1)
        positions = jnp.cumsum(routed.astype(jnp.int32), dtype=jnp.int32) - 1
        select = routed[None, :] & (positions[None, :] == slot_ids)
        selects.append(select)
        weights.append(jnp.sum(jnp.where(select, gate_val[None, :], 0.0), axis=1))
    return jnp.concatenate(selects, axis=0), jnp.concatenate(weights)


def pick_rows(select, rows):
    return jnp.dot(select.astype(rows.dtype), rows, preferred_element_type=jnp.float32).astype(rows.dtype)


def halve_over_et(parts, order, hook):
    n = lax.axis_size("et")
    me = lax.axis_index("et")
    remaining = sorted(order)
    held = parts
    for bit in order[:-1]:
        lower = 1 << remaining.index(bit)
        count = held.shape[0]
        halves = held.reshape((count // (2 * lower), 2, lower) + held.shape[1:])
        side = (me // bit) % 2
        keep = jnp.take(halves, side, axis=1).reshape((count // 2,) + held.shape[1:])
        give = jnp.take(halves, 1 - side, axis=1).reshape((count // 2,) + held.shape[1:])
        got = lax.ppermute(give, "et", [(i, i ^ bit) for i in range(n)])
        held = (keep.astype(jnp.float32) + got.astype(jnp.float32)).astype(jnp.bfloat16)
        held = hook(held)
        hook = lambda value: value
        remaining.remove(bit)
    bit = order[-1]
    side = (me // bit) % 2
    return jnp.take(held, side, axis=0), jnp.take(held, 1 - side, axis=0), bit


def round_order(n, late):
    bits = [1 << k for k in range(n.bit_length() - 1)]
    if late in bits:
        bits = [bit for bit in bits if bit != late] + [late]
    return bits


def reduce_to_owner(parts, order, hook):
    n = lax.axis_size("et")
    keep, give, bit = halve_over_et(parts, order, hook)
    got = lax.ppermute(give, "et", [(i, i ^ bit) for i in range(n)])
    return keep.astype(jnp.float32) + got.astype(jnp.float32)


def reduce_to_previous(parts, order, hook):
    n = lax.axis_size("et")
    stages = lax.axis_size("pipe")
    keep, give, bit = halve_over_et(parts, order, hook)
    to_same = [(stage * n + i, (stage - 1) * n + i) for stage in range(1, stages) for i in range(n)]
    to_other = [(stage * n + i, (stage - 1) * n + (i ^ bit)) for stage in range(1, stages) for i in range(n)]
    first = lax.ppermute(keep, ("pipe", "et"), to_same)
    second = lax.ppermute(give, ("pipe", "et"), to_other)
    return first.astype(jnp.float32) + second.astype(jnp.float32)


def unpack(slot_sums, select):
    return lax.dot_general(
        select.astype(jnp.float32),
        slot_sums,
        (((0,), (0,)), ((), ())),
        precision=lax.Precision.HIGHEST,
        preferred_element_type=jnp.float32,
    ).astype(jnp.bfloat16)


def _expert_body(x_ref, g_ref, w_ref, wg_ref, wu_ref, wd_ref, out_ref, grad_ref, out_acc, grad_acc):
    step = pl.program_id(1)
    rows = x_ref.shape[0] * x_ref.shape[1]
    width = x_ref.shape[2]

    @pl.when(step == 0)
    def _():
        out_acc[...] = jnp.zeros_like(out_acc)
        grad_acc[...] = jnp.zeros_like(grad_acc)

    x = x_ref[...].reshape(rows, width)
    g = g_ref[...].reshape(rows, width)
    gate_w = w_ref[...].reshape(rows, w_ref.shape[2])[:, 0:1].astype(jnp.float32)
    wg = wg_ref[...]
    wu = wu_ref[...]
    wd = wd_ref[...]
    pre_gate = jnp.dot(x, wg, preferred_element_type=jnp.float32)
    pre_up = jnp.dot(x, wu, preferred_element_type=jnp.float32)
    d_hidden = gate_w * lax.dot_general(g, wd, (((1,), (1,)), ((), ())), preferred_element_type=jnp.float32)
    sigma = jax.nn.sigmoid(pre_gate)
    activated = pre_gate * sigma
    slopes = sigma * (1.0 + pre_gate * (1.0 - sigma))
    hidden = (activated * pre_up).astype(jnp.bfloat16)
    out_acc[...] += jnp.dot(hidden, wd, preferred_element_type=jnp.float32)
    d_gate = (d_hidden * pre_up * slopes).astype(jnp.bfloat16)
    d_up = (d_hidden * activated).astype(jnp.bfloat16)
    grad_acc[...] += lax.dot_general(
        d_gate, wg, (((1,), (1,)), ((), ())), preferred_element_type=jnp.float32
    ) + lax.dot_general(d_up, wu, (((1,), (1,)), ((), ())), preferred_element_type=jnp.float32)

    @pl.when(step == pl.num_programs(1) - 1)
    def _():
        out_ref[...] = (gate_w * out_acc[...]).astype(out_ref.dtype).reshape(out_ref.shape)
        grad_ref[...] = grad_acc[...].astype(grad_ref.dtype).reshape(grad_ref.shape)


def expert_pass(gathered, gate_mats, up_mats, down_mats):
    n, experts, most, packed_width = gathered.shape
    width = gate_mats.shape[1]
    shard = gate_mats.shape[2]
    tile = shard
    steps = shard // tile
    rows = n * most
    return pl.pallas_call(
        _expert_body,
        grid=(experts, steps),
        in_specs=[
            pl.BlockSpec((n, None, most, width), lambda e, f: (0, e, 0, 0)),
            pl.BlockSpec((n, None, most, width), lambda e, f: (0, e, 0, 1)),
            pl.BlockSpec((n, None, most, TAIL), lambda e, f: (0, e, 0, 2 * width // TAIL)),
            pl.BlockSpec((None, width, tile), lambda e, f: (e, 0, f)),
            pl.BlockSpec((None, width, tile), lambda e, f: (e, 0, f)),
            pl.BlockSpec((None, tile, width), lambda e, f: (e, f, 0)),
        ],
        out_specs=[
            pl.BlockSpec((n, None, most, width), lambda e, f: (0, e, 0, 0)),
            pl.BlockSpec((n, None, most, width), lambda e, f: (0, e, 0, 0)),
        ],
        out_shape=[
            jax.ShapeDtypeStruct((n, experts, most, width), jnp.bfloat16),
            jax.ShapeDtypeStruct((n, experts, most, width), jnp.bfloat16),
        ],
        scratch_shapes=[pltpu.VMEM((rows, width), jnp.float32), pltpu.VMEM((rows, width), jnp.float32)],
        compiler_params=pltpu.CompilerParams(
            dimension_semantics=("arbitrary", "arbitrary"), vmem_limit_bytes=100 * 1024 * 1024
        ),
    )(gathered, gathered, gathered, gate_mats, up_mats, down_mats)


def per_device(tokens, gate_vals, expert_ids, grad_out, w_gate, w_up, w_down):
    local_rows = tokens[0]
    local_grads = grad_out[0]
    gate_mats = w_gate[0]
    up_mats = w_up[0]
    down_mats = w_down[0]
    n = lax.axis_size("et")
    width = local_rows.shape[1]
    select, weights = local_slots(expert_ids[0], gate_vals[0])
    next_routes = shifted(expert_ids[0], "pipe", -1)
    next_select = local_slots(next_routes, gate_vals[0])[0]
    weight_cols = jnp.broadcast_to(weights.astype(jnp.bfloat16)[:, None], (E_WIN * MOST, TAIL))
    packed = jnp.concatenate(
        [pick_rows(select, local_rows), pick_rows(select, local_grads), weight_cols], axis=1
    )
    gathered = lax.all_gather(packed, "et", axis=0, tiled=True).reshape(n, E_WIN, MOST, 2 * width + TAIL)
    out_parts, grad_parts = expert_pass(gathered, gate_mats, up_mats, down_mats)
    same = lambda value: value
    out_sums = reduce_to_owner(out_parts.reshape(n, E_WIN * MOST, width), round_order(n, n // 2), same)
    received = unpack(
        reduce_to_previous(grad_parts.reshape(n, E_WIN * MOST, width), round_order(n, 2), same), next_select
    )
    out_share = unpack(out_sums, select)
    return (out_share[None], received[None])


def solution(mesh):
    placed = (
        P("pipe", "et", None),
        P("pipe", "et", None),
        P("pipe", "et", None),
        P("pipe", "et", None),
        P("pipe", None, None, "et"),
        P("pipe", None, None, "et"),
        P("pipe", None, "et", None),
    )
    return jax.shard_map(
        per_device,
        mesh=mesh,
        in_specs=placed,
        out_specs=(P("pipe", "et", None), P("pipe", "et", None)),
        check_vma=False,
    )
```

```python
import jax
import jax.numpy as jnp
from jax import lax
from jax.experimental import pallas as pl
from jax.experimental.pallas import tpu as pltpu
from jax.sharding import PartitionSpec as P

E_WIN = 2
MOST = 16
TAIL = 128


def shifted(value, axis, steps):
    count = lax.axis_size(axis)
    first, last = (max(0, -steps), min(count, count - steps))
    return lax.ppermute(value, axis, [(source, source + steps) for source in range(first, last)])


def silu_parts(pre_gate):
    sigma = jax.nn.sigmoid(pre_gate)
    return (pre_gate * sigma, sigma * (1.0 + pre_gate * (1.0 - sigma)))


def local_slots(local_routes, local_gates):
    slot_ids = jnp.arange(MOST, dtype=jnp.int32)[:, None]
    selects, weights = [], []
    for expert in range(E_WIN):
        matches = local_routes == expert
        routed = jnp.any(matches, axis=1)
        gate_val = jnp.sum(jnp.where(matches, local_gates.astype(jnp.float32), 0.0), axis=1)
        positions = jnp.cumsum(routed.astype(jnp.int32), dtype=jnp.int32) - 1
        select = routed[None, :] & (positions[None, :] == slot_ids)
        selects.append(select)
        weights.append(jnp.sum(jnp.where(select, gate_val[None, :], 0.0), axis=1))
    return jnp.concatenate(selects, axis=0), jnp.concatenate(weights)


def pick_rows(select, rows):
    return jnp.dot(select.astype(rows.dtype), rows, preferred_element_type=jnp.float32).astype(rows.dtype)


def swap(value, bit):
    n = lax.axis_size("et")
    return lax.ppermute(value, "et", [(i, i ^ bit) for i in range(n)])


def gather_over_et(packed):
    n = lax.axis_size("et")
    if n == 8:
        pair = jnp.stack([packed, swap(packed, 1)])
        across_x = swap(pair, 2)
        across_y = swap(pair, 4)
        last_x = swap(across_y[0], 2)
        last_y = swap(across_x[1], 4)
        return jnp.concatenate([pair, across_x, across_y, last_x[None], last_y[None]], axis=0)
    held = packed[None]
    bit = 1
    while bit < n:
        held = jnp.concatenate([held, swap(held, bit)], axis=0)
        bit *= 2
    return held


def halve_over_et(parts, order, hook):
    n = lax.axis_size("et")
    me = lax.axis_index("et")
    remaining = sorted(order)
    held = parts
    for bit in order[:-1]:
        lower = 1 << remaining.index(bit)
        count = held.shape[0]
        halves = held.reshape((count // (2 * lower), 2, lower) + held.shape[1:])
        keep = halves[:, 0].reshape((count // 2,) + held.shape[1:])
        give = halves[:, 1].reshape((count // 2,) + held.shape[1:])
        got = lax.ppermute(give, "et", [(i, i ^ bit) for i in range(n)])
        held = (keep.astype(jnp.float32) + got.astype(jnp.float32)).astype(jnp.bfloat16)
        held = hook(held)
        hook = lambda value: value
        remaining.remove(bit)
    bit = order[-1]
    return held[0], held[1], bit


def round_order(n, late):
    bits = [1 << k for k in range(n.bit_length() - 1)]
    if late in bits:
        bits = [bit for bit in bits if bit != late] + [late]
    return bits


def reduce_to_owner(parts, order, hook):
    n = lax.axis_size("et")
    keep, give, bit = halve_over_et(parts, order, hook)
    got = lax.ppermute(give, "et", [(i, i ^ bit) for i in range(n)])
    return keep.astype(jnp.float32) + got.astype(jnp.float32)


def reduce_to_previous(parts, order, hook):
    n = lax.axis_size("et")
    stages = lax.axis_size("pipe")
    keep, give, bit = halve_over_et(parts, order, hook)
    to_same = [(stage * n + i, (stage - 1) * n + i) for stage in range(1, stages) for i in range(n)]
    to_other = [(stage * n + i, (stage - 1) * n + (i ^ bit)) for stage in range(1, stages) for i in range(n)]
    first = lax.ppermute(keep, ("pipe", "et"), to_same)
    second = lax.ppermute(give, ("pipe", "et"), to_other)
    return first.astype(jnp.float32) + second.astype(jnp.float32)


def unpack(slot_sums, select):
    return lax.dot_general(
        select.astype(jnp.float32),
        slot_sums,
        (((0,), (0,)), ((), ())),
        precision=lax.Precision.HIGHEST,
        preferred_element_type=jnp.float32,
    ).astype(jnp.bfloat16)


def _expert_body(x_ref, g_ref, w_ref, wg_ref, wu_ref, wd_ref, out_ref, grad_ref, out_acc, grad_acc):
    step = pl.program_id(1)
    rows = x_ref.shape[0] * x_ref.shape[1]
    width = x_ref.shape[2]

    @pl.when(step == 0)
    def _():
        out_acc[...] = jnp.zeros_like(out_acc)
        grad_acc[...] = jnp.zeros_like(grad_acc)

    x = x_ref[...].reshape(rows, width)
    g = g_ref[...].reshape(rows, width)
    gate_w = w_ref[...].reshape(rows, w_ref.shape[2])[:, 0:1].astype(jnp.float32)
    wg = wg_ref[...]
    wu = wu_ref[...]
    wd = wd_ref[...]
    pre_gate = jnp.dot(x, wg, preferred_element_type=jnp.float32)
    pre_up = jnp.dot(x, wu, preferred_element_type=jnp.float32)
    d_hidden = gate_w * lax.dot_general(g, wd, (((1,), (1,)), ((), ())), preferred_element_type=jnp.float32)
    sigma = jax.nn.sigmoid(pre_gate)
    activated = pre_gate * sigma
    slopes = sigma * (1.0 + pre_gate * (1.0 - sigma))
    hidden = (activated * pre_up).astype(jnp.bfloat16)
    out_acc[...] += jnp.dot(hidden, wd, preferred_element_type=jnp.float32)
    d_gate = (d_hidden * pre_up * slopes).astype(jnp.bfloat16)
    d_up = (d_hidden * activated).astype(jnp.bfloat16)
    grad_acc[...] += lax.dot_general(
        d_gate, wg, (((1,), (1,)), ((), ())), preferred_element_type=jnp.float32
    ) + lax.dot_general(d_up, wu, (((1,), (1,)), ((), ())), preferred_element_type=jnp.float32)

    @pl.when(step == pl.num_programs(1) - 1)
    def _():
        out_ref[...] = (gate_w * out_acc[...]).astype(out_ref.dtype).reshape(out_ref.shape)
        grad_ref[...] = grad_acc[...].astype(grad_ref.dtype).reshape(grad_ref.shape)


def expert_pass(gathered, gate_mats, up_mats, down_mats):
    n, experts, most, packed_width = gathered.shape
    width = gate_mats.shape[1]
    shard = gate_mats.shape[2]
    tile = shard
    steps = shard // tile
    rows = n * most
    return pl.pallas_call(
        _expert_body,
        grid=(experts, steps),
        in_specs=[
            pl.BlockSpec((n, None, most, width), lambda e, f: (0, e, 0, 0)),
            pl.BlockSpec((n, None, most, width), lambda e, f: (0, e, 0, 1)),
            pl.BlockSpec((n, None, most, TAIL), lambda e, f: (0, e, 0, 2 * width // TAIL)),
            pl.BlockSpec((None, width, tile), lambda e, f: (e, 0, f)),
            pl.BlockSpec((None, width, tile), lambda e, f: (e, 0, f)),
            pl.BlockSpec((None, tile, width), lambda e, f: (e, f, 0)),
        ],
        out_specs=[
            pl.BlockSpec((n, None, most, width), lambda e, f: (0, e, 0, 0)),
            pl.BlockSpec((n, None, most, width), lambda e, f: (0, e, 0, 0)),
        ],
        out_shape=[
            jax.ShapeDtypeStruct((n, experts, most, width), jnp.bfloat16),
            jax.ShapeDtypeStruct((n, experts, most, width), jnp.bfloat16),
        ],
        scratch_shapes=[pltpu.VMEM((rows, width), jnp.float32), pltpu.VMEM((rows, width), jnp.float32)],
        compiler_params=pltpu.CompilerParams(
            dimension_semantics=("arbitrary", "arbitrary"), vmem_limit_bytes=100 * 1024 * 1024
        ),
    )(gathered, gathered, gathered, gate_mats, up_mats, down_mats)


def per_device(tokens, gate_vals, expert_ids, grad_out, w_gate, w_up, w_down):
    local_rows = tokens[0]
    local_grads = grad_out[0]
    gate_mats = w_gate[0]
    up_mats = w_up[0]
    down_mats = w_down[0]
    n = lax.axis_size("et")
    width = local_rows.shape[1]
    select, weights = local_slots(expert_ids[0], gate_vals[0])
    next_routes = shifted(expert_ids[0], "pipe", -1)
    next_select = local_slots(next_routes, gate_vals[0])[0]
    weight_cols = jnp.broadcast_to(weights.astype(jnp.bfloat16)[:, None], (E_WIN * MOST, TAIL))
    packed = jnp.concatenate(
        [pick_rows(select, local_rows), pick_rows(select, local_grads), weight_cols], axis=1
    )
    gathered = gather_over_et(packed).reshape(n, E_WIN, MOST, 2 * width + TAIL)
    out_parts, grad_parts = expert_pass(gathered, gate_mats, up_mats, down_mats)
    same = lambda value: value
    out_sums = reduce_to_owner(out_parts.reshape(n, E_WIN * MOST, width), round_order(n, n // 2), same)
    received = unpack(
        reduce_to_previous(grad_parts.reshape(n, E_WIN * MOST, width), round_order(n, 2), same), next_select
    )
    out_share = unpack(out_sums, select)
    return (out_share[None], received[None])


def solution(mesh):
    placed = (
        P("pipe", "et", None),
        P("pipe", "et", None),
        P("pipe", "et", None),
        P("pipe", "et", None),
        P("pipe", None, None, "et"),
        P("pipe", None, None, "et"),
        P("pipe", None, "et", None),
    )
    return jax.shard_map(
        per_device,
        mesh=mesh,
        in_specs=placed,
        out_specs=(P("pipe", "et", None), P("pipe", "et", None)),
        check_vma=False,
    )
```

```python
import jax
import jax.numpy as jnp
from jax import lax
from jax.experimental import pallas as pl
from jax.experimental.pallas import tpu as pltpu
from jax.sharding import PartitionSpec as P

E_WIN = 2
MOST = 16
TAIL = 128


def shifted(value, axis, steps):
    count = lax.axis_size(axis)
    first, last = (max(0, -steps), min(count, count - steps))
    return lax.ppermute(value, axis, [(source, source + steps) for source in range(first, last)])


def silu_parts(pre_gate):
    sigma = jax.nn.sigmoid(pre_gate)
    return (pre_gate * sigma, sigma * (1.0 + pre_gate * (1.0 - sigma)))


def local_slots(local_routes, local_gates):
    slot_ids = jnp.arange(MOST, dtype=jnp.int32)[:, None]
    selects, weights = [], []
    for expert in range(E_WIN):
        matches = local_routes == expert
        routed = jnp.any(matches, axis=1)
        gate_val = jnp.sum(jnp.where(matches, local_gates.astype(jnp.float32), 0.0), axis=1)
        positions = jnp.cumsum(routed.astype(jnp.int32), dtype=jnp.int32) - 1
        select = routed[None, :] & (positions[None, :] == slot_ids)
        selects.append(select)
        weights.append(jnp.sum(jnp.where(select, gate_val[None, :], 0.0), axis=1))
    return jnp.concatenate(selects, axis=0), jnp.concatenate(weights)


def pick_rows(select, rows):
    return jnp.dot(select.astype(rows.dtype), rows, preferred_element_type=jnp.float32).astype(rows.dtype)


def swap(value, bit):
    n = lax.axis_size("et")
    return lax.ppermute(value, "et", [(i, i ^ bit) for i in range(n)])


def gather_over_et(packed):
    n = lax.axis_size("et")
    if n == 8:
        core = swap(packed, 1)
        near_x = swap(packed, 2)
        near_y = swap(packed, 4)
        third = swap(core, 2)
        fifth = swap(core, 4)
        sixth = swap(near_y, 2)
        seventh = swap(sixth, 1)
        return jnp.stack([packed, core, near_x, third, near_y, fifth, sixth, seventh])
    held = packed[None]
    bit = 1
    while bit < n:
        held = jnp.concatenate([held, swap(held, bit)], axis=0)
        bit *= 2
    return held


def halve_over_et(parts, order, hook):
    n = lax.axis_size("et")
    me = lax.axis_index("et")
    remaining = sorted(order)
    held = parts
    for bit in order[:-1]:
        lower = 1 << remaining.index(bit)
        count = held.shape[0]
        halves = held.reshape((count // (2 * lower), 2, lower) + held.shape[1:])
        keep = halves[:, 0].reshape((count // 2,) + held.shape[1:])
        give = halves[:, 1].reshape((count // 2,) + held.shape[1:])
        got = lax.ppermute(give, "et", [(i, i ^ bit) for i in range(n)])
        held = (keep.astype(jnp.float32) + got.astype(jnp.float32)).astype(jnp.bfloat16)
        held = hook(held)
        hook = lambda value: value
        remaining.remove(bit)
    bit = order[-1]
    return held[0], held[1], bit


def round_order(n, late):
    bits = [1 << k for k in range(n.bit_length() - 1)]
    if late in bits:
        bits = [bit for bit in bits if bit != late] + [late]
    return bits


def reduce_to_owner(parts, order, hook):
    n = lax.axis_size("et")
    keep, give, bit = halve_over_et(parts, order, hook)
    got = lax.ppermute(give, "et", [(i, i ^ bit) for i in range(n)])
    return keep.astype(jnp.float32) + got.astype(jnp.float32)


def reduce_to_previous(parts, order, hook):
    n = lax.axis_size("et")
    stages = lax.axis_size("pipe")
    keep, give, bit = halve_over_et(parts, order, hook)
    to_same = [(stage * n + i, (stage - 1) * n + i) for stage in range(1, stages) for i in range(n)]
    to_other = [(stage * n + i, (stage - 1) * n + (i ^ bit)) for stage in range(1, stages) for i in range(n)]
    first = lax.ppermute(keep, ("pipe", "et"), to_same)
    second = lax.ppermute(give, ("pipe", "et"), to_other)
    return first.astype(jnp.float32) + second.astype(jnp.float32)


def unpack(slot_sums, select):
    return lax.dot_general(
        select.astype(jnp.float32),
        slot_sums,
        (((0,), (0,)), ((), ())),
        precision=lax.Precision.HIGHEST,
        preferred_element_type=jnp.float32,
    ).astype(jnp.bfloat16)


def _expert_body(x_ref, g_ref, w_ref, wg_ref, wu_ref, wd_ref, out_ref, grad_ref, out_acc, grad_acc):
    step = pl.program_id(1)
    rows = x_ref.shape[0] * x_ref.shape[1]
    width = x_ref.shape[2]

    @pl.when(step == 0)
    def _():
        out_acc[...] = jnp.zeros_like(out_acc)
        grad_acc[...] = jnp.zeros_like(grad_acc)

    x = x_ref[...].reshape(rows, width)
    g = g_ref[...].reshape(rows, width)
    gate_w = w_ref[...].reshape(rows, w_ref.shape[2])[:, 0:1].astype(jnp.float32)
    wg = wg_ref[...]
    wu = wu_ref[...]
    wd = wd_ref[...]
    pre_gate = jnp.dot(x, wg, preferred_element_type=jnp.float32)
    pre_up = jnp.dot(x, wu, preferred_element_type=jnp.float32)
    d_hidden = gate_w * lax.dot_general(g, wd, (((1,), (1,)), ((), ())), preferred_element_type=jnp.float32)
    sigma = jax.nn.sigmoid(pre_gate)
    activated = pre_gate * sigma
    slopes = sigma * (1.0 + pre_gate * (1.0 - sigma))
    hidden = (activated * pre_up).astype(jnp.bfloat16)
    out_acc[...] += jnp.dot(hidden, wd, preferred_element_type=jnp.float32)
    d_gate = (d_hidden * pre_up * slopes).astype(jnp.bfloat16)
    d_up = (d_hidden * activated).astype(jnp.bfloat16)
    grad_acc[...] += lax.dot_general(
        d_gate, wg, (((1,), (1,)), ((), ())), preferred_element_type=jnp.float32
    ) + lax.dot_general(d_up, wu, (((1,), (1,)), ((), ())), preferred_element_type=jnp.float32)

    @pl.when(step == pl.num_programs(1) - 1)
    def _():
        out_ref[...] = (gate_w * out_acc[...]).astype(out_ref.dtype).reshape(out_ref.shape)
        grad_ref[...] = grad_acc[...].astype(grad_ref.dtype).reshape(grad_ref.shape)


def expert_pass(gathered, gate_mats, up_mats, down_mats):
    n, experts, most, packed_width = gathered.shape
    width = gate_mats.shape[1]
    shard = gate_mats.shape[2]
    tile = shard
    steps = shard // tile
    rows = n * most
    return pl.pallas_call(
        _expert_body,
        grid=(experts, steps),
        in_specs=[
            pl.BlockSpec((n, None, most, width), lambda e, f: (0, e, 0, 0)),
            pl.BlockSpec((n, None, most, width), lambda e, f: (0, e, 0, 1)),
            pl.BlockSpec((n, None, most, TAIL), lambda e, f: (0, e, 0, 2 * width // TAIL)),
            pl.BlockSpec((None, width, tile), lambda e, f: (e, 0, f)),
            pl.BlockSpec((None, width, tile), lambda e, f: (e, 0, f)),
            pl.BlockSpec((None, tile, width), lambda e, f: (e, f, 0)),
        ],
        out_specs=[
            pl.BlockSpec((n, None, most, width), lambda e, f: (0, e, 0, 0)),
            pl.BlockSpec((n, None, most, width), lambda e, f: (0, e, 0, 0)),
        ],
        out_shape=[
            jax.ShapeDtypeStruct((n, experts, most, width), jnp.bfloat16),
            jax.ShapeDtypeStruct((n, experts, most, width), jnp.bfloat16),
        ],
        scratch_shapes=[pltpu.VMEM((rows, width), jnp.float32), pltpu.VMEM((rows, width), jnp.float32)],
        compiler_params=pltpu.CompilerParams(
            dimension_semantics=("arbitrary", "arbitrary"), vmem_limit_bytes=100 * 1024 * 1024
        ),
    )(gathered, gathered, gathered, gate_mats, up_mats, down_mats)


def per_device(tokens, gate_vals, expert_ids, grad_out, w_gate, w_up, w_down):
    local_rows = tokens[0]
    local_grads = grad_out[0]
    gate_mats = w_gate[0]
    up_mats = w_up[0]
    down_mats = w_down[0]
    n = lax.axis_size("et")
    width = local_rows.shape[1]
    select, weights = local_slots(expert_ids[0], gate_vals[0])
    next_routes = shifted(expert_ids[0], "pipe", -1)
    next_select = local_slots(next_routes, gate_vals[0])[0]
    weight_cols = jnp.broadcast_to(weights.astype(jnp.bfloat16)[:, None], (E_WIN * MOST, TAIL))
    packed = jnp.concatenate(
        [pick_rows(select, local_rows), pick_rows(select, local_grads), weight_cols], axis=1
    )
    gathered = gather_over_et(packed).reshape(n, E_WIN, MOST, 2 * width + TAIL)
    out_parts, grad_parts = expert_pass(gathered, gate_mats, up_mats, down_mats)
    same = lambda value: value
    out_sums = reduce_to_owner(out_parts.reshape(n, E_WIN * MOST, width), round_order(n, n // 2), same)
    received = unpack(
        reduce_to_previous(grad_parts.reshape(n, E_WIN * MOST, width), round_order(n, 2), same), next_select
    )
    out_share = unpack(out_sums, select)
    return (out_share[None], received[None])


def solution(mesh):
    placed = (
        P("pipe", "et", None),
        P("pipe", "et", None),
        P("pipe", "et", None),
        P("pipe", "et", None),
        P("pipe", None, None, "et"),
        P("pipe", None, None, "et"),
        P("pipe", None, "et", None),
    )
    return jax.shard_map(
        per_device,
        mesh=mesh,
        in_specs=placed,
        out_specs=(P("pipe", "et", None), P("pipe", "et", None)),
        check_vma=False,
    )
```

```python
import jax
import jax.numpy as jnp
from jax import lax
from jax.experimental import pallas as pl
from jax.experimental.pallas import tpu as pltpu
from jax.sharding import PartitionSpec as P

E_WIN = 2
MOST = 16
TAIL = 128


def shifted(value, axis, steps):
    count = lax.axis_size(axis)
    first, last = (max(0, -steps), min(count, count - steps))
    return lax.ppermute(value, axis, [(source, source + steps) for source in range(first, last)])


def silu_parts(pre_gate):
    sigma = jax.nn.sigmoid(pre_gate)
    return (pre_gate * sigma, sigma * (1.0 + pre_gate * (1.0 - sigma)))


def local_slots(local_routes, local_gates):
    slot_ids = jnp.arange(MOST, dtype=jnp.int32)[:, None]
    selects, weights = [], []
    for expert in range(E_WIN):
        matches = local_routes == expert
        routed = jnp.any(matches, axis=1)
        gate_val = jnp.sum(jnp.where(matches, local_gates.astype(jnp.float32), 0.0), axis=1)
        positions = jnp.cumsum(routed.astype(jnp.int32), dtype=jnp.int32) - 1
        select = routed[None, :] & (positions[None, :] == slot_ids)
        selects.append(select)
        weights.append(jnp.sum(jnp.where(select, gate_val[None, :], 0.0), axis=1))
    return jnp.concatenate(selects, axis=0), jnp.concatenate(weights)


def pick_rows(select, rows):
    return jnp.dot(select.astype(rows.dtype), rows, preferred_element_type=jnp.float32).astype(rows.dtype)


def swap(value, bit):
    n = lax.axis_size("et")
    return lax.ppermute(value, "et", [(i, i ^ bit) for i in range(n)])


def gather_over_et(packed):
    n = lax.axis_size("et")
    if n == 8:
        core = swap(packed, 1)
        near_x = swap(packed, 2)
        near_y = swap(packed, 4)
        third = swap(core, 2)
        fifth = swap(core, 4)
        half = packed.shape[0] // 2
        sixth = jnp.concatenate([swap(near_y[:half], 2), swap(near_x[half:], 4)], axis=0)
        seventh = swap(sixth, 1)
        return jnp.stack([packed, core, near_x, third, near_y, fifth, sixth, seventh])
    held = packed[None]
    bit = 1
    while bit < n:
        held = jnp.concatenate([held, swap(held, bit)], axis=0)
        bit *= 2
    return held


def halve_over_et(parts, order, hook):
    n = lax.axis_size("et")
    me = lax.axis_index("et")
    remaining = sorted(order)
    held = parts
    for bit in order[:-1]:
        lower = 1 << remaining.index(bit)
        count = held.shape[0]
        halves = held.reshape((count // (2 * lower), 2, lower) + held.shape[1:])
        keep = halves[:, 0].reshape((count // 2,) + held.shape[1:])
        give = halves[:, 1].reshape((count // 2,) + held.shape[1:])
        got = lax.ppermute(give, "et", [(i, i ^ bit) for i in range(n)])
        held = (keep.astype(jnp.float32) + got.astype(jnp.float32)).astype(jnp.bfloat16)
        held = hook(held)
        hook = lambda value: value
        remaining.remove(bit)
    bit = order[-1]
    return held[0], held[1], bit


def round_order(n, late):
    bits = [1 << k for k in range(n.bit_length() - 1)]
    if late in bits:
        bits = [bit for bit in bits if bit != late] + [late]
    return bits


def reduce_to_owner(parts, order, hook):
    n = lax.axis_size("et")
    keep, give, bit = halve_over_et(parts, order, hook)
    got = lax.ppermute(give, "et", [(i, i ^ bit) for i in range(n)])
    return keep.astype(jnp.float32) + got.astype(jnp.float32)


def reduce_to_previous(parts, order, hook):
    n = lax.axis_size("et")
    stages = lax.axis_size("pipe")
    keep, give, bit = halve_over_et(parts, order, hook)
    to_same = [(stage * n + i, (stage - 1) * n + i) for stage in range(1, stages) for i in range(n)]
    to_other = [(stage * n + i, (stage - 1) * n + (i ^ bit)) for stage in range(1, stages) for i in range(n)]
    first = lax.ppermute(keep, ("pipe", "et"), to_same)
    second = lax.ppermute(give, ("pipe", "et"), to_other)
    return first.astype(jnp.float32) + second.astype(jnp.float32)


def unpack(slot_sums, select):
    return lax.dot_general(
        select.astype(jnp.float32),
        slot_sums,
        (((0,), (0,)), ((), ())),
        precision=lax.Precision.HIGHEST,
        preferred_element_type=jnp.float32,
    ).astype(jnp.bfloat16)


def _expert_body(x_ref, g_ref, w_ref, wg_ref, wu_ref, wd_ref, out_ref, grad_ref, out_acc, grad_acc):
    step = pl.program_id(1)
    rows = x_ref.shape[0] * x_ref.shape[1]
    width = x_ref.shape[2]

    @pl.when(step == 0)
    def _():
        out_acc[...] = jnp.zeros_like(out_acc)
        grad_acc[...] = jnp.zeros_like(grad_acc)

    x = x_ref[...].reshape(rows, width)
    g = g_ref[...].reshape(rows, width)
    gate_w = w_ref[...].reshape(rows, w_ref.shape[2])[:, 0:1].astype(jnp.float32)
    wg = wg_ref[...]
    wu = wu_ref[...]
    wd = wd_ref[...]
    pre_gate = jnp.dot(x, wg, preferred_element_type=jnp.float32)
    pre_up = jnp.dot(x, wu, preferred_element_type=jnp.float32)
    d_hidden = gate_w * lax.dot_general(g, wd, (((1,), (1,)), ((), ())), preferred_element_type=jnp.float32)
    sigma = jax.nn.sigmoid(pre_gate)
    activated = pre_gate * sigma
    slopes = sigma * (1.0 + pre_gate * (1.0 - sigma))
    hidden = (activated * pre_up).astype(jnp.bfloat16)
    out_acc[...] += jnp.dot(hidden, wd, preferred_element_type=jnp.float32)
    d_gate = (d_hidden * pre_up * slopes).astype(jnp.bfloat16)
    d_up = (d_hidden * activated).astype(jnp.bfloat16)
    grad_acc[...] += lax.dot_general(
        d_gate, wg, (((1,), (1,)), ((), ())), preferred_element_type=jnp.float32
    ) + lax.dot_general(d_up, wu, (((1,), (1,)), ((), ())), preferred_element_type=jnp.float32)

    @pl.when(step == pl.num_programs(1) - 1)
    def _():
        out_ref[...] = (gate_w * out_acc[...]).astype(out_ref.dtype).reshape(out_ref.shape)
        grad_ref[...] = grad_acc[...].astype(grad_ref.dtype).reshape(grad_ref.shape)


def expert_pass(gathered, gate_mats, up_mats, down_mats):
    n, experts, most, packed_width = gathered.shape
    width = gate_mats.shape[1]
    shard = gate_mats.shape[2]
    tile = shard
    steps = shard // tile
    rows = n * most
    return pl.pallas_call(
        _expert_body,
        grid=(experts, steps),
        in_specs=[
            pl.BlockSpec((n, None, most, width), lambda e, f: (0, e, 0, 0)),
            pl.BlockSpec((n, None, most, width), lambda e, f: (0, e, 0, 1)),
            pl.BlockSpec((n, None, most, TAIL), lambda e, f: (0, e, 0, 2 * width // TAIL)),
            pl.BlockSpec((None, width, tile), lambda e, f: (e, 0, f)),
            pl.BlockSpec((None, width, tile), lambda e, f: (e, 0, f)),
            pl.BlockSpec((None, tile, width), lambda e, f: (e, f, 0)),
        ],
        out_specs=[
            pl.BlockSpec((n, None, most, width), lambda e, f: (0, e, 0, 0)),
            pl.BlockSpec((n, None, most, width), lambda e, f: (0, e, 0, 0)),
        ],
        out_shape=[
            jax.ShapeDtypeStruct((n, experts, most, width), jnp.bfloat16),
            jax.ShapeDtypeStruct((n, experts, most, width), jnp.bfloat16),
        ],
        scratch_shapes=[pltpu.VMEM((rows, width), jnp.float32), pltpu.VMEM((rows, width), jnp.float32)],
        compiler_params=pltpu.CompilerParams(
            dimension_semantics=("arbitrary", "arbitrary"), vmem_limit_bytes=100 * 1024 * 1024
        ),
    )(gathered, gathered, gathered, gate_mats, up_mats, down_mats)


def per_device(tokens, gate_vals, expert_ids, grad_out, w_gate, w_up, w_down):
    local_rows = tokens[0]
    local_grads = grad_out[0]
    gate_mats = w_gate[0]
    up_mats = w_up[0]
    down_mats = w_down[0]
    n = lax.axis_size("et")
    width = local_rows.shape[1]
    select, weights = local_slots(expert_ids[0], gate_vals[0])
    next_routes = shifted(expert_ids[0], "pipe", -1)
    next_select = local_slots(next_routes, gate_vals[0])[0]
    weight_cols = jnp.broadcast_to(weights.astype(jnp.bfloat16)[:, None], (E_WIN * MOST, TAIL))
    packed = jnp.concatenate(
        [pick_rows(select, local_rows), pick_rows(select, local_grads), weight_cols], axis=1
    )
    gathered = gather_over_et(packed).reshape(n, E_WIN, MOST, 2 * width + TAIL)
    out_parts, grad_parts = expert_pass(gathered, gate_mats, up_mats, down_mats)
    same = lambda value: value
    out_sums = reduce_to_owner(out_parts.reshape(n, E_WIN * MOST, width), round_order(n, n // 2), same)
    received = unpack(
        reduce_to_previous(grad_parts.reshape(n, E_WIN * MOST, width), round_order(n, 2), same), next_select
    )
    out_share = unpack(out_sums, select)
    return (out_share[None], received[None])


def solution(mesh):
    placed = (
        P("pipe", "et", None),
        P("pipe", "et", None),
        P("pipe", "et", None),
        P("pipe", "et", None),
        P("pipe", None, None, "et"),
        P("pipe", None, None, "et"),
        P("pipe", None, "et", None),
    )
    return jax.shard_map(
        per_device,
        mesh=mesh,
        in_specs=placed,
        out_specs=(P("pipe", "et", None), P("pipe", "et", None)),
        check_vma=False,
    )
```

```python
import jax
import jax.numpy as jnp
from jax import lax
from jax.experimental import pallas as pl
from jax.experimental.pallas import tpu as pltpu
from jax.sharding import PartitionSpec as P

E_WIN = 2
MOST = 16
TAIL = 128


def shifted(value, axis, steps):
    count = lax.axis_size(axis)
    first, last = (max(0, -steps), min(count, count - steps))
    return lax.ppermute(value, axis, [(source, source + steps) for source in range(first, last)])


def silu_parts(pre_gate):
    sigma = jax.nn.sigmoid(pre_gate)
    return (pre_gate * sigma, sigma * (1.0 + pre_gate * (1.0 - sigma)))


def local_slots(local_routes, local_gates):
    slot_ids = jnp.arange(MOST, dtype=jnp.int32)[:, None]
    selects, weights = [], []
    for expert in range(E_WIN):
        matches = local_routes == expert
        routed = jnp.any(matches, axis=1)
        gate_val = jnp.sum(jnp.where(matches, local_gates.astype(jnp.float32), 0.0), axis=1)
        positions = jnp.cumsum(routed.astype(jnp.int32), dtype=jnp.int32) - 1
        select = routed[None, :] & (positions[None, :] == slot_ids)
        selects.append(select)
        weights.append(jnp.sum(jnp.where(select, gate_val[None, :], 0.0), axis=1))
    return jnp.concatenate(selects, axis=0), jnp.concatenate(weights)


def pick_rows(select, rows):
    return jnp.dot(select.astype(rows.dtype), rows, preferred_element_type=jnp.float32).astype(rows.dtype)


def swap(value, bit):
    n = lax.axis_size("et")
    return lax.ppermute(value, "et", [(i, i ^ bit) for i in range(n)])


def gather_over_et(packed):
    n = lax.axis_size("et")
    if n == 8:
        core = swap(packed, 1)
        near_x = swap(packed, 2)
        near_y = swap(packed, 4)
        third = swap(core, 2)
        fifth = swap(core, 4)
        half = packed.shape[0] // 2
        sixth = jnp.concatenate([swap(near_y[:half], 2), swap(near_x[half:], 4)], axis=0)
        seventh = swap(sixth, 1)
        return jnp.stack([packed, core, near_x, third, near_y, fifth, sixth, seventh])
    held = packed[None]
    bit = 1
    while bit < n:
        held = jnp.concatenate([held, swap(held, bit)], axis=0)
        bit *= 2
    return held


def halve_over_et(parts, order, hook):
    n = lax.axis_size("et")
    me = lax.axis_index("et")
    remaining = sorted(order)
    held = parts
    for bit in order[:-1]:
        lower = 1 << remaining.index(bit)
        count = held.shape[0]
        halves = held.reshape((count // (2 * lower), 2, lower) + held.shape[1:])
        keep = halves[:, 0].reshape((count // 2,) + held.shape[1:])
        give = halves[:, 1].reshape((count // 2,) + held.shape[1:])
        got = lax.ppermute(give, "et", [(i, i ^ bit) for i in range(n)])
        held = (keep.astype(jnp.float32) + got.astype(jnp.float32)).astype(jnp.bfloat16)
        held = hook(held)
        hook = lambda value: value
        remaining.remove(bit)
    bit = order[-1]
    return held[0], held[1], bit


def round_order(n, late):
    bits = [1 << k for k in range(n.bit_length() - 1)]
    if late in bits:
        bits = [bit for bit in bits if bit != late] + [late]
    return bits


def reduce_to_owner(parts, order, hook):
    n = lax.axis_size("et")
    keep, give, bit = halve_over_et(parts, order, hook)
    got = lax.ppermute(give, "et", [(i, i ^ bit) for i in range(n)])
    return keep.astype(jnp.float32) + got.astype(jnp.float32)


def reduce_to_previous(parts, order, hook):
    n = lax.axis_size("et")
    stages = lax.axis_size("pipe")
    keep, give, bit = halve_over_et(parts, order, hook)
    to_same = [(stage * n + i, (stage - 1) * n + i) for stage in range(1, stages) for i in range(n)]
    to_other = [(stage * n + i, (stage - 1) * n + (i ^ bit)) for stage in range(1, stages) for i in range(n)]
    first = lax.ppermute(keep, ("pipe", "et"), to_same)
    second = lax.ppermute(give, ("pipe", "et"), to_other)
    return first.astype(jnp.float32) + second.astype(jnp.float32)


def unpack(slot_sums, select):
    return lax.dot_general(
        select.astype(jnp.float32),
        slot_sums,
        (((0,), (0,)), ((), ())),
        precision=lax.Precision.HIGHEST,
        preferred_element_type=jnp.float32,
    ).astype(jnp.bfloat16)


def _expert_body(x_ref, g_ref, w_ref, wg_ref, wu_ref, wd_ref, out_ref, grad_ref, out_acc, grad_acc):
    step = pl.program_id(1)
    rows = x_ref.shape[0] * x_ref.shape[1]
    width = x_ref.shape[2]

    @pl.when(step == 0)
    def _():
        out_acc[...] = jnp.zeros_like(out_acc)
        grad_acc[...] = jnp.zeros_like(grad_acc)

    x = x_ref[...].reshape(rows, width)
    g = g_ref[...].reshape(rows, width)
    gate_w = w_ref[...].reshape(rows, w_ref.shape[2])[:, 0:1].astype(jnp.float32)
    wg = wg_ref[...]
    wu = wu_ref[...]
    wd = wd_ref[...]
    pre_gate = jnp.dot(x, wg, preferred_element_type=jnp.float32)
    pre_up = jnp.dot(x, wu, preferred_element_type=jnp.float32)
    d_hidden = gate_w * lax.dot_general(g, wd, (((1,), (1,)), ((), ())), preferred_element_type=jnp.float32)
    sigma = jax.nn.sigmoid(pre_gate)
    activated = pre_gate * sigma
    slopes = sigma * (1.0 + pre_gate * (1.0 - sigma))
    hidden = (activated * pre_up).astype(jnp.bfloat16)
    out_acc[...] += jnp.dot(hidden, wd, preferred_element_type=jnp.float32)
    d_gate = (d_hidden * pre_up * slopes).astype(jnp.bfloat16)
    d_up = (d_hidden * activated).astype(jnp.bfloat16)
    grad_acc[...] += lax.dot_general(
        d_gate, wg, (((1,), (1,)), ((), ())), preferred_element_type=jnp.float32
    ) + lax.dot_general(d_up, wu, (((1,), (1,)), ((), ())), preferred_element_type=jnp.float32)

    @pl.when(step == pl.num_programs(1) - 1)
    def _():
        out_ref[...] = (gate_w * out_acc[...]).astype(out_ref.dtype).reshape(out_ref.shape)
        grad_ref[...] = grad_acc[...].astype(grad_ref.dtype).reshape(grad_ref.shape)


def expert_pass(gathered, gate_mats, up_mats, down_mats):
    n, experts, most, packed_width = gathered.shape
    width = gate_mats.shape[1]
    shard = gate_mats.shape[2]
    tile = shard
    steps = shard // tile
    rows = n * most
    return pl.pallas_call(
        _expert_body,
        grid=(experts, steps),
        in_specs=[
            pl.BlockSpec((n, None, most, width), lambda e, f: (0, e, 0, 0)),
            pl.BlockSpec((n, None, most, width), lambda e, f: (0, e, 0, 1)),
            pl.BlockSpec((n, None, most, TAIL), lambda e, f: (0, e, 0, 2 * width // TAIL)),
            pl.BlockSpec((None, width, tile), lambda e, f: (e, 0, f)),
            pl.BlockSpec((None, width, tile), lambda e, f: (e, 0, f)),
            pl.BlockSpec((None, tile, width), lambda e, f: (e, f, 0)),
        ],
        out_specs=[
            pl.BlockSpec((n, None, most, width), lambda e, f: (0, e, 0, 0)),
            pl.BlockSpec((n, None, most, width), lambda e, f: (0, e, 0, 0)),
        ],
        out_shape=[
            jax.ShapeDtypeStruct((n, experts, most, width), jnp.bfloat16),
            jax.ShapeDtypeStruct((n, experts, most, width), jnp.bfloat16),
        ],
        scratch_shapes=[pltpu.VMEM((rows, width), jnp.float32), pltpu.VMEM((rows, width), jnp.float32)],
        compiler_params=pltpu.CompilerParams(
            dimension_semantics=("arbitrary", "arbitrary"), vmem_limit_bytes=100 * 1024 * 1024
        ),
    )(gathered, gathered, gathered, gate_mats, up_mats, down_mats)


def per_device(tokens, gate_vals, expert_ids, grad_out, w_gate, w_up, w_down):
    local_rows = tokens[0]
    local_grads = grad_out[0]
    gate_mats = w_gate[0]
    up_mats = w_up[0]
    down_mats = w_down[0]
    n = lax.axis_size("et")
    width = local_rows.shape[1]
    select, weights = local_slots(expert_ids[0], gate_vals[0])
    next_routes = shifted(expert_ids[0], "pipe", -1)
    next_select = local_slots(next_routes, gate_vals[0])[0]
    weight_cols = jnp.broadcast_to(weights.astype(jnp.bfloat16)[:, None], (E_WIN * MOST, TAIL))
    packed = jnp.concatenate(
        [pick_rows(select, local_rows), pick_rows(select, local_grads), weight_cols], axis=1
    )
    gathered = gather_over_et(packed).reshape(n, E_WIN, MOST, 2 * width + TAIL)
    out_parts, grad_parts = expert_pass(gathered, gate_mats, up_mats, down_mats)
    same = lambda value: value
    slots = E_WIN * MOST
    both = jnp.concatenate(
        [out_parts.reshape(n, slots, width), grad_parts.reshape(n, slots, width)], axis=1
    ).reshape(n // 2, 2, 2 * slots, width)
    merged = swap(both[:, 1], 1)
    held = (both[:, 0].astype(jnp.float32) + merged.astype(jnp.float32)).astype(jnp.bfloat16)
    out_order = [bit for bit in round_order(n, n // 2) if bit != 1]
    grad_order = [bit for bit in round_order(n, 2) if bit != 1]
    out_sums = reduce_to_owner(held[:, :slots], out_order, same)
    received = unpack(reduce_to_previous(held[:, slots:], grad_order, same), next_select)
    out_share = unpack(out_sums, select)
    return (out_share[None], received[None])


def solution(mesh):
    placed = (
        P("pipe", "et", None),
        P("pipe", "et", None),
        P("pipe", "et", None),
        P("pipe", "et", None),
        P("pipe", None, None, "et"),
        P("pipe", None, None, "et"),
        P("pipe", None, "et", None),
    )
    return jax.shard_map(
        per_device,
        mesh=mesh,
        in_specs=placed,
        out_specs=(P("pipe", "et", None), P("pipe", "et", None)),
        check_vma=False,
    )
```

```python
import jax
import jax.numpy as jnp
from jax import lax
from jax.experimental import pallas as pl
from jax.experimental.pallas import tpu as pltpu
from jax.sharding import PartitionSpec as P

E_WIN = 2
MOST = 16
TAIL = 128


def shifted(value, axis, steps):
    count = lax.axis_size(axis)
    first, last = (max(0, -steps), min(count, count - steps))
    return lax.ppermute(value, axis, [(source, source + steps) for source in range(first, last)])


def silu_parts(pre_gate):
    sigma = jax.nn.sigmoid(pre_gate)
    return (pre_gate * sigma, sigma * (1.0 + pre_gate * (1.0 - sigma)))


def local_slots(local_routes, local_gates):
    slot_ids = jnp.arange(MOST, dtype=jnp.int32)[:, None]
    selects, weights = [], []
    for expert in range(E_WIN):
        matches = local_routes == expert
        routed = jnp.any(matches, axis=1)
        gate_val = jnp.sum(jnp.where(matches, local_gates.astype(jnp.float32), 0.0), axis=1)
        positions = jnp.cumsum(routed.astype(jnp.int32), dtype=jnp.int32) - 1
        select = routed[None, :] & (positions[None, :] == slot_ids)
        selects.append(select)
        weights.append(jnp.sum(jnp.where(select, gate_val[None, :], 0.0), axis=1))
    return jnp.concatenate(selects, axis=0), jnp.concatenate(weights)


def pick_rows(select, rows):
    return jnp.dot(select.astype(rows.dtype), rows, preferred_element_type=jnp.float32).astype(rows.dtype)


def swap(value, bit):
    n = lax.axis_size("et")
    return lax.ppermute(value, "et", [(i, i ^ bit) for i in range(n)])


def gather_over_et(packed):
    n = lax.axis_size("et")
    if n == 8:
        core = swap(packed, 1)
        near_x = swap(packed, 2)
        near_y = swap(packed, 4)
        third = swap(core, 2)
        fifth = swap(core, 4)
        half = packed.shape[0] // 2
        sixth = jnp.concatenate([swap(near_y[:half], 2), swap(near_x[half:], 4)], axis=0)
        seventh = swap(sixth, 1)
        return jnp.stack([packed, core, near_x, third, near_y, fifth, sixth, seventh])
    held = packed[None]
    bit = 1
    while bit < n:
        held = jnp.concatenate([held, swap(held, bit)], axis=0)
        bit *= 2
    return held


def halve_over_et(parts, order, hook):
    n = lax.axis_size("et")
    me = lax.axis_index("et")
    remaining = sorted(order)
    held = parts
    for bit in order[:-1]:
        lower = 1 << remaining.index(bit)
        count = held.shape[0]
        halves = held.reshape((count // (2 * lower), 2, lower) + held.shape[1:])
        keep = halves[:, 0].reshape((count // 2,) + held.shape[1:])
        give = halves[:, 1].reshape((count // 2,) + held.shape[1:])
        got = lax.ppermute(give, "et", [(i, i ^ bit) for i in range(n)])
        held = (keep.astype(jnp.float32) + got.astype(jnp.float32)).astype(jnp.bfloat16)
        held = hook(held)
        hook = lambda value: value
        remaining.remove(bit)
    bit = order[-1]
    return held[0], held[1], bit


def round_order(n, late):
    bits = [1 << k for k in range(n.bit_length() - 1)]
    if late in bits:
        bits = [bit for bit in bits if bit != late] + [late]
    return bits


def reduce_to_owner(parts, order, hook):
    n = lax.axis_size("et")
    keep, give, bit = halve_over_et(parts, order, hook)
    got = lax.ppermute(give, "et", [(i, i ^ bit) for i in range(n)])
    return keep.astype(jnp.float32) + got.astype(jnp.float32)


def reduce_to_previous(parts, order, hook):
    n = lax.axis_size("et")
    stages = lax.axis_size("pipe")
    keep, give, bit = halve_over_et(parts, order, hook)
    to_same = [(stage * n + i, (stage - 1) * n + i) for stage in range(1, stages) for i in range(n)]
    to_other = [(stage * n + i, (stage - 1) * n + (i ^ bit)) for stage in range(1, stages) for i in range(n)]
    first = lax.ppermute(keep, ("pipe", "et"), to_same)
    second = lax.ppermute(give, ("pipe", "et"), to_other)
    return first.astype(jnp.float32) + second.astype(jnp.float32)


def unpack(slot_sums, select):
    return lax.dot_general(
        select.astype(jnp.float32),
        slot_sums,
        (((0,), (0,)), ((), ())),
        precision=lax.Precision.HIGHEST,
        preferred_element_type=jnp.float32,
    ).astype(jnp.bfloat16)


def _expert_body(x_ref, g_ref, w_ref, wg_ref, wu_ref, wd_ref, out_ref, grad_ref, out_acc, grad_acc):
    step = pl.program_id(1)
    rows = x_ref.shape[0] * x_ref.shape[1]
    width = x_ref.shape[2]

    @pl.when(step == 0)
    def _():
        out_acc[...] = jnp.zeros_like(out_acc)
        grad_acc[...] = jnp.zeros_like(grad_acc)

    x = x_ref[...].reshape(rows, width)
    g = g_ref[...].reshape(rows, width)
    gate_w = w_ref[...].reshape(rows, w_ref.shape[2])[:, 0:1].astype(jnp.float32)
    wg = wg_ref[...]
    wu = wu_ref[...]
    wd = wd_ref[...]
    pre_gate = jnp.dot(x, wg, preferred_element_type=jnp.float32)
    pre_up = jnp.dot(x, wu, preferred_element_type=jnp.float32)
    d_hidden = gate_w * lax.dot_general(g, wd, (((1,), (1,)), ((), ())), preferred_element_type=jnp.float32)
    sigma = jax.nn.sigmoid(pre_gate)
    activated = pre_gate * sigma
    slopes = sigma * (1.0 + pre_gate * (1.0 - sigma))
    hidden = (activated * pre_up).astype(jnp.bfloat16)
    out_acc[...] += jnp.dot(hidden, wd, preferred_element_type=jnp.float32)
    d_gate = (d_hidden * pre_up * slopes).astype(jnp.bfloat16)
    d_up = (d_hidden * activated).astype(jnp.bfloat16)
    grad_acc[...] += lax.dot_general(
        d_gate, wg, (((1,), (1,)), ((), ())), preferred_element_type=jnp.float32
    ) + lax.dot_general(d_up, wu, (((1,), (1,)), ((), ())), preferred_element_type=jnp.float32)

    @pl.when(step == pl.num_programs(1) - 1)
    def _():
        out_ref[...] = (gate_w * out_acc[...]).astype(out_ref.dtype).reshape(out_ref.shape)
        grad_ref[...] = grad_acc[...].astype(grad_ref.dtype).reshape(grad_ref.shape)


def expert_pass(gathered, gate_mats, up_mats, down_mats):
    n, experts, most, packed_width = gathered.shape
    width = gate_mats.shape[1]
    shard = gate_mats.shape[2]
    tile = shard
    steps = shard // tile
    rows = n * most
    return pl.pallas_call(
        _expert_body,
        grid=(experts, steps),
        in_specs=[
            pl.BlockSpec((n, None, most, width), lambda e, f: (0, e, 0, 0)),
            pl.BlockSpec((n, None, most, width), lambda e, f: (0, e, 0, 1)),
            pl.BlockSpec((n, None, most, TAIL), lambda e, f: (0, e, 0, 2 * width // TAIL)),
            pl.BlockSpec((None, width, tile), lambda e, f: (e, 0, f)),
            pl.BlockSpec((None, width, tile), lambda e, f: (e, 0, f)),
            pl.BlockSpec((None, tile, width), lambda e, f: (e, f, 0)),
        ],
        out_specs=[
            pl.BlockSpec((n, None, most, width), lambda e, f: (0, e, 0, 0)),
            pl.BlockSpec((n, None, most, width), lambda e, f: (0, e, 0, 0)),
        ],
        out_shape=[
            jax.ShapeDtypeStruct((n, experts, most, width), jnp.bfloat16),
            jax.ShapeDtypeStruct((n, experts, most, width), jnp.bfloat16),
        ],
        scratch_shapes=[pltpu.VMEM((rows, width), jnp.float32), pltpu.VMEM((rows, width), jnp.float32)],
        compiler_params=pltpu.CompilerParams(
            dimension_semantics=("arbitrary", "arbitrary"), vmem_limit_bytes=100 * 1024 * 1024
        ),
    )(gathered, gathered, gathered, gate_mats, up_mats, down_mats)


def per_device(tokens, gate_vals, expert_ids, grad_out, w_gate, w_up, w_down):
    local_rows = tokens[0]
    local_grads = grad_out[0]
    gate_mats = w_gate[0]
    up_mats = w_up[0]
    down_mats = w_down[0]
    n = lax.axis_size("et")
    width = local_rows.shape[1]
    select, weights = local_slots(expert_ids[0], gate_vals[0])
    next_routes = shifted(expert_ids[0], "pipe", -1)
    next_select = local_slots(next_routes, gate_vals[0])[0]
    weight_cols = jnp.broadcast_to(weights.astype(jnp.bfloat16)[:, None], (E_WIN * MOST, TAIL))
    packed = jnp.concatenate(
        [pick_rows(select, local_rows), pick_rows(select, local_grads), weight_cols], axis=1
    )
    gathered = gather_over_et(packed).reshape(n, E_WIN, MOST, 2 * width + TAIL)
    out_parts, grad_parts = expert_pass(gathered, gate_mats, up_mats, down_mats)
    same = lambda value: value
    out_sums = reduce_to_owner(out_parts.reshape(n, E_WIN * MOST, width), round_order(n, 2), same)
    received = unpack(
        reduce_to_previous(grad_parts.reshape(n, E_WIN * MOST, width), round_order(n, n // 2), same), next_select
    )
    out_share = unpack(out_sums, select)
    return (out_share[None], received[None])


def solution(mesh):
    placed = (
        P("pipe", "et", None),
        P("pipe", "et", None),
        P("pipe", "et", None),
        P("pipe", "et", None),
        P("pipe", None, None, "et"),
        P("pipe", None, None, "et"),
        P("pipe", None, "et", None),
    )
    return jax.shard_map(
        per_device,
        mesh=mesh,
        in_specs=placed,
        out_specs=(P("pipe", "et", None), P("pipe", "et", None)),
        check_vma=False,
    )
```

```python
import jax
import jax.numpy as jnp
from jax import lax
from jax.experimental import pallas as pl
from jax.experimental.pallas import tpu as pltpu
from jax.sharding import PartitionSpec as P

E_WIN = 2
MOST = 16
TAIL = 128


def shifted(value, axis, steps):
    count = lax.axis_size(axis)
    first, last = (max(0, -steps), min(count, count - steps))
    return lax.ppermute(value, axis, [(source, source + steps) for source in range(first, last)])


def silu_parts(pre_gate):
    sigma = jax.nn.sigmoid(pre_gate)
    return (pre_gate * sigma, sigma * (1.0 + pre_gate * (1.0 - sigma)))


def local_slots(local_routes, local_gates):
    slot_ids = jnp.arange(MOST, dtype=jnp.int32)[:, None]
    selects, weights = [], []
    for expert in range(E_WIN):
        matches = local_routes == expert
        routed = jnp.any(matches, axis=1)
        gate_val = jnp.sum(jnp.where(matches, local_gates.astype(jnp.float32), 0.0), axis=1)
        positions = jnp.cumsum(routed.astype(jnp.int32), dtype=jnp.int32) - 1
        select = routed[None, :] & (positions[None, :] == slot_ids)
        selects.append(select)
        weights.append(jnp.sum(jnp.where(select, gate_val[None, :], 0.0), axis=1))
    return jnp.concatenate(selects, axis=0), jnp.concatenate(weights)


def pick_rows(select, rows):
    return jnp.dot(select.astype(rows.dtype), rows, preferred_element_type=jnp.float32).astype(rows.dtype)


def swap(value, bit):
    n = lax.axis_size("et")
    return lax.ppermute(value, "et", [(i, i ^ bit) for i in range(n)])


def gather_over_et(packed):
    n = lax.axis_size("et")
    if n == 8:
        core = swap(packed, 1)
        near_x = swap(packed, 2)
        near_y = swap(packed, 4)
        third = swap(core, 2)
        fifth = swap(core, 4)
        half = packed.shape[0] // 2
        sixth = jnp.concatenate([swap(near_y[:half], 2), swap(near_x[half:], 4)], axis=0)
        seventh = swap(sixth, 1)
        return jnp.stack([packed, core, near_x, third, near_y, fifth, sixth, seventh])
    held = packed[None]
    bit = 1
    while bit < n:
        held = jnp.concatenate([held, swap(held, bit)], axis=0)
        bit *= 2
    return held


def halve_over_et(parts, order, hook):
    n = lax.axis_size("et")
    me = lax.axis_index("et")
    remaining = sorted(order)
    held = parts
    for bit in order[:-1]:
        lower = 1 << remaining.index(bit)
        count = held.shape[0]
        halves = held.reshape((count // (2 * lower), 2, lower) + held.shape[1:])
        keep = halves[:, 0].reshape((count // 2,) + held.shape[1:])
        give = halves[:, 1].reshape((count // 2,) + held.shape[1:])
        got = lax.ppermute(give, "et", [(i, i ^ bit) for i in range(n)])
        held = (keep.astype(jnp.float32) + got.astype(jnp.float32)).astype(jnp.bfloat16)
        held = hook(held)
        hook = lambda value: value
        remaining.remove(bit)
    bit = order[-1]
    return held[0], held[1], bit


def round_order(n, late):
    bits = [1 << k for k in range(n.bit_length() - 1)]
    if late in bits:
        bits = [bit for bit in bits if bit != late] + [late]
    return bits


def reduce_to_owner(parts, order, hook):
    n = lax.axis_size("et")
    keep, give, bit = halve_over_et(parts, order, hook)
    got = lax.ppermute(give, "et", [(i, i ^ bit) for i in range(n)])
    return keep.astype(jnp.float32) + got.astype(jnp.float32)


def reduce_to_previous(parts, order, hook):
    n = lax.axis_size("et")
    stages = lax.axis_size("pipe")
    keep, give, bit = halve_over_et(parts, order, hook)
    to_same = [(stage * n + i, (stage - 1) * n + i) for stage in range(1, stages) for i in range(n)]
    to_other = [(stage * n + i, (stage - 1) * n + (i ^ bit)) for stage in range(1, stages) for i in range(n)]
    first = lax.ppermute(keep, ("pipe", "et"), to_same)
    second = lax.ppermute(give, ("pipe", "et"), to_other)
    return first.astype(jnp.float32) + second.astype(jnp.float32)


def unpack(slot_sums, select):
    return lax.dot_general(
        select.astype(jnp.float32),
        slot_sums,
        (((0,), (0,)), ((), ())),
        precision=lax.Precision.HIGH,
        preferred_element_type=jnp.float32,
    ).astype(jnp.bfloat16)


def _expert_body(x_ref, g_ref, w_ref, wg_ref, wu_ref, wd_ref, out_ref, grad_ref, out_acc, grad_acc):
    step = pl.program_id(1)
    rows = x_ref.shape[0] * x_ref.shape[1]
    width = x_ref.shape[2]

    @pl.when(step == 0)
    def _():
        out_acc[...] = jnp.zeros_like(out_acc)
        grad_acc[...] = jnp.zeros_like(grad_acc)

    x = x_ref[...].reshape(rows, width)
    g = g_ref[...].reshape(rows, width)
    gate_w = w_ref[...].reshape(rows, w_ref.shape[2])[:, 0:1].astype(jnp.float32)
    wg = wg_ref[...]
    wu = wu_ref[...]
    wd = wd_ref[...]
    pre_gate = jnp.dot(x, wg, preferred_element_type=jnp.float32)
    pre_up = jnp.dot(x, wu, preferred_element_type=jnp.float32)
    d_hidden = gate_w * lax.dot_general(g, wd, (((1,), (1,)), ((), ())), preferred_element_type=jnp.float32)
    sigma = jax.nn.sigmoid(pre_gate)
    activated = pre_gate * sigma
    slopes = sigma * (1.0 + pre_gate * (1.0 - sigma))
    hidden = (activated * pre_up).astype(jnp.bfloat16)
    out_acc[...] += jnp.dot(hidden, wd, preferred_element_type=jnp.float32)
    d_gate = (d_hidden * pre_up * slopes).astype(jnp.bfloat16)
    d_up = (d_hidden * activated).astype(jnp.bfloat16)
    grad_acc[...] += lax.dot_general(
        d_gate, wg, (((1,), (1,)), ((), ())), preferred_element_type=jnp.float32
    ) + lax.dot_general(d_up, wu, (((1,), (1,)), ((), ())), preferred_element_type=jnp.float32)

    @pl.when(step == pl.num_programs(1) - 1)
    def _():
        out_ref[...] = (gate_w * out_acc[...]).astype(out_ref.dtype).reshape(out_ref.shape)
        grad_ref[...] = grad_acc[...].astype(grad_ref.dtype).reshape(grad_ref.shape)


def expert_pass(gathered, gate_mats, up_mats, down_mats):
    n, experts, most, packed_width = gathered.shape
    width = gate_mats.shape[1]
    shard = gate_mats.shape[2]
    tile = shard
    steps = shard // tile
    rows = n * most
    return pl.pallas_call(
        _expert_body,
        grid=(experts, steps),
        in_specs=[
            pl.BlockSpec((n, None, most, width), lambda e, f: (0, e, 0, 0)),
            pl.BlockSpec((n, None, most, width), lambda e, f: (0, e, 0, 1)),
            pl.BlockSpec((n, None, most, TAIL), lambda e, f: (0, e, 0, 2 * width // TAIL)),
            pl.BlockSpec((None, width, tile), lambda e, f: (e, 0, f)),
            pl.BlockSpec((None, width, tile), lambda e, f: (e, 0, f)),
            pl.BlockSpec((None, tile, width), lambda e, f: (e, f, 0)),
        ],
        out_specs=[
            pl.BlockSpec((n, None, most, width), lambda e, f: (0, e, 0, 0)),
            pl.BlockSpec((n, None, most, width), lambda e, f: (0, e, 0, 0)),
        ],
        out_shape=[
            jax.ShapeDtypeStruct((n, experts, most, width), jnp.bfloat16),
            jax.ShapeDtypeStruct((n, experts, most, width), jnp.bfloat16),
        ],
        scratch_shapes=[pltpu.VMEM((rows, width), jnp.float32), pltpu.VMEM((rows, width), jnp.float32)],
        compiler_params=pltpu.CompilerParams(
            dimension_semantics=("arbitrary", "arbitrary"), vmem_limit_bytes=100 * 1024 * 1024
        ),
    )(gathered, gathered, gathered, gate_mats, up_mats, down_mats)


def per_device(tokens, gate_vals, expert_ids, grad_out, w_gate, w_up, w_down):
    local_rows = tokens[0]
    local_grads = grad_out[0]
    gate_mats = w_gate[0]
    up_mats = w_up[0]
    down_mats = w_down[0]
    n = lax.axis_size("et")
    width = local_rows.shape[1]
    select, weights = local_slots(expert_ids[0], gate_vals[0])
    next_routes = shifted(expert_ids[0], "pipe", -1)
    next_select = local_slots(next_routes, gate_vals[0])[0]
    weight_cols = jnp.broadcast_to(weights.astype(jnp.bfloat16)[:, None], (E_WIN * MOST, TAIL))
    packed = jnp.concatenate(
        [pick_rows(select, local_rows), pick_rows(select, local_grads), weight_cols], axis=1
    )
    gathered = gather_over_et(packed).reshape(n, E_WIN, MOST, 2 * width + TAIL)
    out_parts, grad_parts = expert_pass(gathered, gate_mats, up_mats, down_mats)
    same = lambda value: value
    out_sums = reduce_to_owner(out_parts.reshape(n, E_WIN * MOST, width), round_order(n, n // 2), same)
    received = unpack(
        reduce_to_previous(grad_parts.reshape(n, E_WIN * MOST, width), round_order(n, 2), same), next_select
    )
    out_share = unpack(out_sums, select)
    return (out_share[None], received[None])


def solution(mesh):
    placed = (
        P("pipe", "et", None),
        P("pipe", "et", None),
        P("pipe", "et", None),
        P("pipe", "et", None),
        P("pipe", None, None, "et"),
        P("pipe", None, None, "et"),
        P("pipe", None, "et", None),
    )
    return jax.shard_map(
        per_device,
        mesh=mesh,
        in_specs=placed,
        out_specs=(P("pipe", "et", None), P("pipe", "et", None)),
        check_vma=False,
    )
```

```python
import jax
import jax.numpy as jnp
from jax import lax
from jax.experimental import pallas as pl
from jax.experimental.pallas import tpu as pltpu
from jax.sharding import PartitionSpec as P

E_WIN = 2
MOST = 16
TAIL = 128


def shifted(value, axis, steps):
    count = lax.axis_size(axis)
    first, last = (max(0, -steps), min(count, count - steps))
    return lax.ppermute(value, axis, [(source, source + steps) for source in range(first, last)])


def silu_parts(pre_gate):
    sigma = jax.nn.sigmoid(pre_gate)
    return (pre_gate * sigma, sigma * (1.0 + pre_gate * (1.0 - sigma)))


def local_slots(local_routes, local_gates):
    slot_ids = jnp.arange(MOST, dtype=jnp.int32)[:, None]
    selects, weights = [], []
    for expert in range(E_WIN):
        matches = local_routes == expert
        routed = jnp.any(matches, axis=1)
        gate_val = jnp.sum(jnp.where(matches, local_gates.astype(jnp.float32), 0.0), axis=1)
        positions = jnp.cumsum(routed.astype(jnp.int32), dtype=jnp.int32) - 1
        select = routed[None, :] & (positions[None, :] == slot_ids)
        selects.append(select)
        weights.append(jnp.sum(jnp.where(select, gate_val[None, :], 0.0), axis=1))
    return jnp.concatenate(selects, axis=0), jnp.concatenate(weights)


def pick_rows(select, rows):
    return jnp.dot(select.astype(rows.dtype), rows, preferred_element_type=jnp.float32).astype(rows.dtype)


def swap(value, bit):
    n = lax.axis_size("et")
    return lax.ppermute(value, "et", [(i, i ^ bit) for i in range(n)])


def gather_over_et(packed):
    n = lax.axis_size("et")
    if n == 8:
        core = swap(packed, 1)
        near_x = swap(packed, 2)
        near_y = swap(packed, 4)
        third = swap(core, 2)
        fifth = swap(core, 4)
        half = packed.shape[0] // 2
        sixth = jnp.concatenate([swap(near_y[:half], 2), swap(near_x[half:], 4)], axis=0)
        seventh = swap(sixth, 1)
        return jnp.stack([packed, core, near_x, third, near_y, fifth, sixth, seventh])
    held = packed[None]
    bit = 1
    while bit < n:
        held = jnp.concatenate([held, swap(held, bit)], axis=0)
        bit *= 2
    return held


def halve_over_et(parts, order, hook):
    n = lax.axis_size("et")
    me = lax.axis_index("et")
    remaining = sorted(order)
    held = parts
    for bit in order[:-1]:
        lower = 1 << remaining.index(bit)
        count = held.shape[0]
        halves = held.reshape((count // (2 * lower), 2, lower) + held.shape[1:])
        keep = halves[:, 0].reshape((count // 2,) + held.shape[1:])
        give = halves[:, 1].reshape((count // 2,) + held.shape[1:])
        got = lax.ppermute(give, "et", [(i, i ^ bit) for i in range(n)])
        held = (keep.astype(jnp.float32) + got.astype(jnp.float32)).astype(jnp.bfloat16)
        held = hook(held)
        hook = lambda value: value
        remaining.remove(bit)
    bit = order[-1]
    return held[0], held[1], bit


def round_order(n, late):
    bits = [1 << k for k in range(n.bit_length() - 1)]
    if late in bits:
        bits = [bit for bit in bits if bit != late] + [late]
    return bits


def reduce_to_owner(parts, order, hook):
    n = lax.axis_size("et")
    keep, give, bit = halve_over_et(parts, order, hook)
    got = lax.ppermute(give, "et", [(i, i ^ bit) for i in range(n)])
    return keep.astype(jnp.float32) + got.astype(jnp.float32)


def reduce_to_previous(parts, order, hook):
    n = lax.axis_size("et")
    stages = lax.axis_size("pipe")
    keep, give, bit = halve_over_et(parts, order, hook)
    to_same = [(stage * n + i, (stage - 1) * n + i) for stage in range(1, stages) for i in range(n)]
    to_other = [(stage * n + i, (stage - 1) * n + (i ^ bit)) for stage in range(1, stages) for i in range(n)]
    first = lax.ppermute(keep, ("pipe", "et"), to_same)
    second = lax.ppermute(give, ("pipe", "et"), to_other)
    return first.astype(jnp.float32) + second.astype(jnp.float32)


def unpack(slot_sums, select):
    high = slot_sums.astype(jnp.bfloat16)
    low = (slot_sums - high.astype(jnp.float32)).astype(jnp.bfloat16)
    picks = select.astype(jnp.bfloat16)
    dims = (((0,), (0,)), ((), ()))
    return (
        lax.dot_general(picks, high, dims, preferred_element_type=jnp.float32)
        + lax.dot_general(picks, low, dims, preferred_element_type=jnp.float32)
    ).astype(jnp.bfloat16)


def _expert_body(x_ref, g_ref, w_ref, wg_ref, wu_ref, wd_ref, out_ref, grad_ref, out_acc, grad_acc):
    step = pl.program_id(1)
    rows = x_ref.shape[0] * x_ref.shape[1]
    width = x_ref.shape[2]

    @pl.when(step == 0)
    def _():
        out_acc[...] = jnp.zeros_like(out_acc)
        grad_acc[...] = jnp.zeros_like(grad_acc)

    x = x_ref[...].reshape(rows, width)
    g = g_ref[...].reshape(rows, width)
    gate_w = w_ref[...].reshape(rows, w_ref.shape[2])[:, 0:1].astype(jnp.float32)
    wg = wg_ref[...]
    wu = wu_ref[...]
    wd = wd_ref[...]
    pre_gate = jnp.dot(x, wg, preferred_element_type=jnp.float32)
    pre_up = jnp.dot(x, wu, preferred_element_type=jnp.float32)
    d_hidden = gate_w * lax.dot_general(g, wd, (((1,), (1,)), ((), ())), preferred_element_type=jnp.float32)
    sigma = jax.nn.sigmoid(pre_gate)
    activated = pre_gate * sigma
    slopes = sigma * (1.0 + pre_gate * (1.0 - sigma))
    hidden = (activated * pre_up).astype(jnp.bfloat16)
    out_acc[...] += jnp.dot(hidden, wd, preferred_element_type=jnp.float32)
    d_gate = (d_hidden * pre_up * slopes).astype(jnp.bfloat16)
    d_up = (d_hidden * activated).astype(jnp.bfloat16)
    grad_acc[...] += lax.dot_general(
        d_gate, wg, (((1,), (1,)), ((), ())), preferred_element_type=jnp.float32
    ) + lax.dot_general(d_up, wu, (((1,), (1,)), ((), ())), preferred_element_type=jnp.float32)

    @pl.when(step == pl.num_programs(1) - 1)
    def _():
        out_ref[...] = (gate_w * out_acc[...]).astype(out_ref.dtype).reshape(out_ref.shape)
        grad_ref[...] = grad_acc[...].astype(grad_ref.dtype).reshape(grad_ref.shape)


def expert_pass(gathered, gate_mats, up_mats, down_mats):
    n, experts, most, packed_width = gathered.shape
    width = gate_mats.shape[1]
    shard = gate_mats.shape[2]
    tile = shard
    steps = shard // tile
    rows = n * most
    return pl.pallas_call(
        _expert_body,
        grid=(experts, steps),
        in_specs=[
            pl.BlockSpec((n, None, most, width), lambda e, f: (0, e, 0, 0)),
            pl.BlockSpec((n, None, most, width), lambda e, f: (0, e, 0, 1)),
            pl.BlockSpec((n, None, most, TAIL), lambda e, f: (0, e, 0, 2 * width // TAIL)),
            pl.BlockSpec((None, width, tile), lambda e, f: (e, 0, f)),
            pl.BlockSpec((None, width, tile), lambda e, f: (e, 0, f)),
            pl.BlockSpec((None, tile, width), lambda e, f: (e, f, 0)),
        ],
        out_specs=[
            pl.BlockSpec((n, None, most, width), lambda e, f: (0, e, 0, 0)),
            pl.BlockSpec((n, None, most, width), lambda e, f: (0, e, 0, 0)),
        ],
        out_shape=[
            jax.ShapeDtypeStruct((n, experts, most, width), jnp.bfloat16),
            jax.ShapeDtypeStruct((n, experts, most, width), jnp.bfloat16),
        ],
        scratch_shapes=[pltpu.VMEM((rows, width), jnp.float32), pltpu.VMEM((rows, width), jnp.float32)],
        compiler_params=pltpu.CompilerParams(
            dimension_semantics=("arbitrary", "arbitrary"), vmem_limit_bytes=100 * 1024 * 1024
        ),
    )(gathered, gathered, gathered, gate_mats, up_mats, down_mats)


def per_device(tokens, gate_vals, expert_ids, grad_out, w_gate, w_up, w_down):
    local_rows = tokens[0]
    local_grads = grad_out[0]
    gate_mats = w_gate[0]
    up_mats = w_up[0]
    down_mats = w_down[0]
    n = lax.axis_size("et")
    width = local_rows.shape[1]
    select, weights = local_slots(expert_ids[0], gate_vals[0])
    next_routes = shifted(expert_ids[0], "pipe", -1)
    next_select = local_slots(next_routes, gate_vals[0])[0]
    weight_cols = jnp.broadcast_to(weights.astype(jnp.bfloat16)[:, None], (E_WIN * MOST, TAIL))
    packed = jnp.concatenate(
        [pick_rows(select, local_rows), pick_rows(select, local_grads), weight_cols], axis=1
    )
    gathered = gather_over_et(packed).reshape(n, E_WIN, MOST, 2 * width + TAIL)
    out_parts, grad_parts = expert_pass(gathered, gate_mats, up_mats, down_mats)
    same = lambda value: value
    out_sums = reduce_to_owner(out_parts.reshape(n, E_WIN * MOST, width), round_order(n, n // 2), same)
    received = unpack(
        reduce_to_previous(grad_parts.reshape(n, E_WIN * MOST, width), round_order(n, 2), same), next_select
    )
    out_share = unpack(out_sums, select)
    return (out_share[None], received[None])


def solution(mesh):
    placed = (
        P("pipe", "et", None),
        P("pipe", "et", None),
        P("pipe", "et", None),
        P("pipe", "et", None),
        P("pipe", None, None, "et"),
        P("pipe", None, None, "et"),
        P("pipe", None, "et", None),
    )
    return jax.shard_map(
        per_device,
        mesh=mesh,
        in_specs=placed,
        out_specs=(P("pipe", "et", None), P("pipe", "et", None)),
        check_vma=False,
    )
```
